256 devices in a mesh: node: 8 (over y, x_lo), gx: 32 (over z, x_hi, core).
Axes of the slice: x: 4 (x_hi: 2, x_lo: 2; x = x_hi * 2 + x_lo), y: 4, z: 8, core: 2. Of those that a mesh axis runs over, the one named last changes fastest.
Arguments:
- start_state: float32 [32, 8, 16, 512], P('gx'), may hold values from -6 to 6
- node_states: float32 [8, 32, 8, 16, 512], P('node', 'gx'), may hold values from -6 to 6
- reaction_rates: float32 [32, 8, 16, 512], P('gx'), may hold values from 0.1 to 1
- volume: bfloat16 [512, 512], replicated, may hold values from -0.25 to 0.25
- face_lift: bfloat16 [384, 512], replicated, may hold values from -0.3125 to 0.3125
Outputs:
- new_states: float32 [8, 32, 8, 16, 512], P('node', 'gx')
The draws below stay inside these ranges and needn't reach their ends.
All inputs are finite; a program needn't handle non-finite values.
Results may differ from the reference program's by a relative error of at most 0.008.
Values may be sent and summed in bfloat16 or wider, within the bound.
No kernel may reach another device: no remote copies, remote signals or barrier semaphores. Data moves between devices by JAX's collectives and lax.ppermute only.
A program may use at most 64 MiB of HBM per device.

```python
import math
import jax
import jax.numpy as jnp
import numpy as np
from jax import lax

M = 8
NP = 8
P_SIZE = 512
EY = 8
EZ = 16
NXE = 32
SWEEPS = 2
INNER = 7


def block_levels(key, shape, cuts, smallest, high):
    def one(position, shards_of):
        draws = jax.random.uniform(jax.random.fold_in(jax.random.fold_in(key, 6), position), (shards_of,), jnp.float32, smallest / len(cuts), high / len(cuts))
        return jnp.repeat(jnp.exp(draws), shape[position] // shards_of).reshape((-1,) + (1,) * (len(shape) - position - 1))

    loudness = one(*cuts[0])
    for cut in cuts[1:]:
        loudness = loudness * one(*cut)
    return loudness


def scatter_about(key, extent, width, bound, shards=(), dtype=jnp.bfloat16):
    loudness = block_levels(key, extent, shards, -0.22, 0.18) if shards else 1.0
    result = jax.random.normal(key, extent, jnp.float32) * width * loudness
    return jnp.minimum(jnp.maximum(result, -bound), bound).astype(dtype)


def setup_inputs(seed: int = 0) -> dict:
    seeds = jax.random.split(jax.random.key(seed), 6)
    return {
        "start_state": scatter_about(seeds[0], (NXE, EY, EZ, P_SIZE), 1.0, 6.0, ((0, 32),), jnp.float32),
        "node_states": scatter_about(seeds[1], (M, NXE, EY, EZ, P_SIZE), 1.0, 6.0, ((0, 8), (1, 32)), jnp.float32),
        "reaction_rates": jnp.clip(jnp.exp(math.log(1.0) - 2.3025851 * jax.random.uniform(seeds[2], (NXE, EY, EZ, P_SIZE), jnp.float32) ** block_levels(seeds[2], (NXE, EY, EZ, P_SIZE), ((0, 32),), -0.2, 0.2)), 0.1, 1.0),
        "volume": scatter_about(seeds[3], (P_SIZE, P_SIZE), (NP**3) ** -0.5, 0.25),
        "face_lift": scatter_about(seeds[4], (6 * NP**2, P_SIZE), (6 * NP**2) ** -0.5, 0.3125),
    }


time_step = 0.45


def quadrature_table(node_count):
    roots_list = []
    for index in range(node_count):
        estimate = math.cos(math.pi * (index + 0.75) / (node_count + 0.5))
        for newton_step in range(60):
            previous, current = 1.0, estimate
            for degree in range(2, node_count + 1):
                previous, current = current, ((2 * degree - 1) * estimate * current - (degree - 1) * previous) / degree
            slope_value = node_count * (estimate * current - previous) / (estimate * estimate - 1.0)
            estimate = estimate - current / slope_value
        roots_list.append(0.5 * (estimate + 1.0))
    times_list = sorted(roots_list)
    weights_table = np.zeros((node_count, node_count))
    for column in range(node_count):
        coeffs = [1.0]
        scaling = 1.0
        for other in range(node_count):
            if other != column:
                point = times_list[other]
                widened = [0.0] * (len(coeffs) + 1)
                for power, entry in enumerate(coeffs):
                    widened[power + 1] += entry
                    widened[power] -= point * entry
                coeffs = widened
                scaling = scaling * (times_list[column] - point)
        for row in range(node_count):
            upper = times_list[row]
            total = 0.0
            for power, entry in enumerate(coeffs):
                total += entry / scaling * upper ** (power + 1) / (power + 1)
            weights_table[row, column] = total
    return np.array(times_list), weights_table


def apply_operator(node_field, reaction_rates, volume, face_lift):
    rounded = node_field.astype(jnp.bfloat16)
    lead_shape = node_field.shape[:-1]
    element_cube = rounded.reshape(lead_shape + (NP, NP, NP))
    face_size = NP * NP
    x_high = element_cube[..., NP - 1, :, :].reshape(lead_shape + (face_size,))
    x_low = element_cube[..., 0, :, :].reshape(lead_shape + (face_size,))
    y_high = element_cube[..., :, NP - 1, :].reshape(lead_shape + (face_size,))
    y_low = element_cube[..., :, 0, :].reshape(lead_shape + (face_size,))
    z_high = element_cube[..., NP - 1].reshape(lead_shape + (face_size,))
    z_low = element_cube[..., 0].reshape(lead_shape + (face_size,))
    gathered = jnp.concatenate([
        jnp.roll(x_high, 1, axis=1), jnp.roll(x_low, -1, axis=1),
        jnp.roll(y_high, 1, axis=2), jnp.roll(y_low, -1, axis=2),
        jnp.roll(z_high, 1, axis=3), jnp.roll(z_low, -1, axis=3)], axis=-1)
    volume_term = jnp.dot(rounded, volume, preferred_element_type=jnp.float32)
    face_term = jnp.dot(gathered, face_lift, preferred_element_type=jnp.float32)
    return volume_term + face_term - reaction_rates * node_field


def reference(start_state, node_states, reaction_rates, volume, face_lift):
    node_times, weights_table = quadrature_table(M)
    all_weights = jnp.asarray(weights_table, jnp.float32)
    own_scales = jnp.asarray(time_step * node_times, jnp.float32).reshape((M, 1, 1, 1, 1))
    states = node_states
    for sweep_index in range(SWEEPS):
        slopes = apply_operator(states, reaction_rates, volume, face_lift)
        slope_rows = slopes.astype(jnp.bfloat16)
        combined = jnp.einsum("mj,jabcp->mabcp", all_weights, slope_rows.astype(jnp.float32), precision=lax.Precision.HIGHEST)
        fixed_part = start_state + time_step * combined - own_scales * slopes
        iterate = start_state + time_step * combined
        for inner_step in range(INNER - 1):
            iterate = fixed_part + own_scales * apply_operator(iterate, reaction_rates, volume, face_lift)
        states = iterate
    return states
```

```python
import math

import jax
import jax.numpy as jnp
import numpy as np
from jax import lax
from jax.sharding import PartitionSpec as P

M = 8
NP = 8
SWEEPS = 2
INNER = 7
FACE = NP * NP


time_step = 0.45


def passed_along(array, axis, by):
    devices = lax.axis_size(axis)
    return lax.ppermute(array, axis, [(i, (i + by) % devices) for i in range(devices)])


def quadrature_table(node_count):
    roots_list = []
    for index in range(node_count):
        estimate = math.cos(math.pi * (index + 0.75) / (node_count + 0.5))
        for newton_step in range(60):
            previous, current = (1.0, estimate)
            for degree in range(2, node_count + 1):
                previous, current = (
                    current,
                    ((2 * degree - 1) * estimate * current - (degree - 1) * previous) / degree,
                )
            slope_value = node_count * (estimate * current - previous) / (estimate * estimate - 1.0)
            estimate = estimate - current / slope_value
        roots_list.append(0.5 * (estimate + 1.0))
    times_list = sorted(roots_list)
    weights_table = np.zeros((node_count, node_count))
    for column in range(node_count):
        coeffs = [1.0]
        scaling = 1.0
        for other in range(node_count):
            if other != column:
                point = times_list[other]
                widened = [0.0] * (len(coeffs) + 1)
                for power, entry in enumerate(coeffs):
                    widened[power + 1] += entry
                    widened[power] -= point * entry
                coeffs = widened
                scaling = scaling * (times_list[column] - point)
        for row in range(node_count):
            upper = times_list[row]
            total = 0.0
            for power, entry in enumerate(coeffs):
                total += entry / scaling * upper ** (power + 1) / (power + 1)
            weights_table[row, column] = total
    return (np.array(times_list), weights_table)


def face_selector(axis, value):
    a, b, c = np.meshgrid(np.arange(NP), np.arange(NP), np.arange(NP), indexing="ij")
    point = ((a * NP + b) * NP + c).reshape(-1)
    keep = [a, b, c][axis].reshape(-1) == value
    select = np.zeros((NP**3, FACE), np.float32)
    select[point[keep], np.arange(FACE)] = 1.0
    return select


def spread_weights(volume, face_lift):
    blocks = [volume]
    for index, (axis, value) in enumerate([(1, NP - 1), (1, 0), (2, NP - 1), (2, 0)]):
        rows = face_lift[(2 + index) * FACE : (3 + index) * FACE]
        select = jnp.asarray(face_selector(axis, value), jnp.bfloat16)
        blocks.append(jnp.dot(select, rows, preferred_element_type=jnp.float32).astype(jnp.bfloat16))
    return jnp.concatenate(blocks, axis=0)


def shifted_inputs(rounded, ny, nz):
    cube = rounded.reshape((ny, nz, -1))
    parts = [
        cube,
        jnp.roll(cube, 1, axis=0),
        jnp.roll(cube, -1, axis=0),
        jnp.roll(cube, 1, axis=1),
        jnp.roll(cube, -1, axis=1),
    ]
    return jnp.concatenate(parts, axis=-1).reshape((ny * nz, -1))


def local_terms(field, reaction, weights, ny, nz):
    rounded = field.astype(jnp.bfloat16)
    stacked = shifted_inputs(rounded, ny, nz)
    own = jnp.dot(stacked, weights, preferred_element_type=jnp.float32) - reaction * field
    return own, rounded


def exchange_faces(rounded):
    high = rounded[:, (NP - 1) * FACE :]
    low = rounded[:, :FACE]
    below = passed_along(high, "gx", 1)
    above = passed_along(low, "gx", -1)
    return jnp.concatenate([below, above], axis=-1)


def apply_operator(field, reaction, weights, x_lift, ny, nz):
    own, rounded = local_terms(field, reaction, weights, ny, nz)
    faces = exchange_faces(rounded)
    return own + jnp.dot(faces, x_lift, preferred_element_type=jnp.float32)


def gather_nodes(rows):
    nodes = lax.axis_size("node")
    me = lax.axis_index("node")
    shifted = [rows] + [passed_along(rows, "node", shift) for shift in range(1, nodes)]
    return shifted, [(me - shift) % nodes for shift in range(nodes)]


def local(start_state, node_states, reaction_rates, volume, face_lift):
    node_times, weights_table = quadrature_table(M)
    shape = node_states.shape
    ny, nz, points = shape[-3], shape[-2], shape[-1]
    rows = ny * nz
    local_count = shape[0]
    first_node = lax.axis_index("node") * local_count
    all_weights = jnp.asarray(weights_table, jnp.float32)
    own_weights = lax.dynamic_slice_in_dim(all_weights, first_node, local_count, 0)
    all_scales = jnp.asarray(time_step * node_times, jnp.float32)
    own_scale = lax.dynamic_slice_in_dim(all_scales, first_node, local_count, 0)[0]

    weights = spread_weights(volume, face_lift)
    x_lift = face_lift[: 2 * FACE]
    start = start_state.reshape((rows, points))
    reaction = reaction_rates.reshape((rows, points))
    states = node_states.reshape((rows, points))
    for sweep_index in range(SWEEPS):
        slopes = apply_operator(states, reaction, weights, x_lift, ny, nz)
        slope_rows = slopes.astype(jnp.bfloat16)
        received, sources = gather_nodes(slope_rows)
        running_sum = jnp.zeros(slopes.shape, jnp.float32)
        for rows_in, source in zip(received, sources):
            running_sum = running_sum + own_weights[0, source] * rows_in.astype(jnp.float32)
        fixed_part = start + time_step * running_sum - own_scale * slopes
        iterate = start + time_step * running_sum
        for inner_step in range(INNER - 1):
            iterate = fixed_part + own_scale * apply_operator(iterate, reaction, weights, x_lift, ny, nz)
        states = iterate
    return states.reshape(shape)


def solution(mesh):
    in_specs = (
        P("gx", None, None, None),
        P("node", "gx", None, None, None),
        P("gx", None, None, None),
        P(),
        P(),
    )
    out_specs = P("node", "gx", None, None, None)
    return jax.shard_map(local, mesh=mesh, in_specs=in_specs, out_specs=out_specs, check_vma=False)
```

```python
import math

import jax
import jax.numpy as jnp
import numpy as np
from jax import lax
from jax.sharding import PartitionSpec as P

M = 8
NP = 8
SWEEPS = 2
INNER = 7
FACE = NP * NP


time_step = 0.45


def passed_along(array, axis, by):
    devices = lax.axis_size(axis)
    return lax.ppermute(array, axis, [(i, (i + by) % devices) for i in range(devices)])


def quadrature_table(node_count):
    roots_list = []
    for index in range(node_count):
        estimate = math.cos(math.pi * (index + 0.75) / (node_count + 0.5))
        for newton_step in range(60):
            previous, current = (1.0, estimate)
            for degree in range(2, node_count + 1):
                previous, current = (
                    current,
                    ((2 * degree - 1) * estimate * current - (degree - 1) * previous) / degree,
                )
            slope_value = node_count * (estimate * current - previous) / (estimate * estimate - 1.0)
            estimate = estimate - current / slope_value
        roots_list.append(0.5 * (estimate + 1.0))
    times_list = sorted(roots_list)
    weights_table = np.zeros((node_count, node_count))
    for column in range(node_count):
        coeffs = [1.0]
        scaling = 1.0
        for other in range(node_count):
            if other != column:
                point = times_list[other]
                widened = [0.0] * (len(coeffs) + 1)
                for power, entry in enumerate(coeffs):
                    widened[power + 1] += entry
                    widened[power] -= point * entry
                coeffs = widened
                scaling = scaling * (times_list[column] - point)
        for row in range(node_count):
            upper = times_list[row]
            total = 0.0
            for power, entry in enumerate(coeffs):
                total += entry / scaling * upper ** (power + 1) / (power + 1)
            weights_table[row, column] = total
    return (np.array(times_list), weights_table)


def face_selector(axis, value):
    a, b, c = np.meshgrid(np.arange(NP), np.arange(NP), np.arange(NP), indexing="ij")
    point = ((a * NP + b) * NP + c).reshape(-1)
    keep = [a, b, c][axis].reshape(-1) == value
    select = np.zeros((NP**3, FACE), np.float32)
    select[point[keep], np.arange(FACE)] = 1.0
    return select


def spread_weights(volume, face_lift):
    blocks = [volume]
    for index, (axis, value) in enumerate([(1, NP - 1), (1, 0), (2, NP - 1), (2, 0)]):
        rows = face_lift[(2 + index) * FACE : (3 + index) * FACE]
        select = jnp.asarray(face_selector(axis, value), jnp.bfloat16)
        blocks.append(jnp.dot(select, rows, preferred_element_type=jnp.float32).astype(jnp.bfloat16))
    return jnp.concatenate(blocks, axis=0)


def shifted_inputs(rounded, ny, nz):
    cube = rounded.reshape((ny, nz, -1))
    parts = [
        cube,
        jnp.roll(cube, 1, axis=0),
        jnp.roll(cube, -1, axis=0),
        jnp.roll(cube, 1, axis=1),
        jnp.roll(cube, -1, axis=1),
    ]
    return jnp.concatenate(parts, axis=-1).reshape((ny * nz, -1))


def local_terms(field, reaction, weights, ny, nz):
    rounded = field.astype(jnp.bfloat16)
    stacked = shifted_inputs(rounded, ny, nz)
    own = jnp.dot(stacked, weights, preferred_element_type=jnp.float32) - reaction * field
    return own, rounded


def exchange_faces(rounded):
    high = rounded[:, (NP - 1) * FACE :]
    low = rounded[:, :FACE]
    below = passed_along(high, "gx", 1)
    above = passed_along(low, "gx", -1)
    return jnp.concatenate([below, above], axis=-1)


def apply_operator(field, reaction, weights, x_lift, ny, nz):
    own, rounded = local_terms(field, reaction, weights, ny, nz)
    faces = exchange_faces(rounded)
    return own + jnp.dot(faces, x_lift, preferred_element_type=jnp.float32)


def two_steps(field, fixed, scale, reaction, weights, x_lift, ny, nz, last_is_slope):
    high_cols = slice((NP - 1) * FACE, NP * FACE)
    low_cols = slice(0, FACE)
    own, rounded = local_terms(field, reaction, weights, ny, nz)
    high = rounded[:, high_cols]
    low = rounded[:, low_cols]
    part_high = fixed[:, high_cols] + scale * own[:, high_cols]
    part_low = fixed[:, low_cols] + scale * own[:, low_cols]
    from_below = passed_along(jnp.concatenate([high.astype(jnp.float32), part_high], -1), "gx", 1)
    from_above = passed_along(jnp.concatenate([low.astype(jnp.float32), part_low], -1), "gx", -1)
    high_2 = passed_along(high, "gx", 2)
    low_2 = passed_along(low, "gx", -2)
    high_1 = from_below[:, :FACE].astype(jnp.bfloat16)
    low_1 = from_above[:, :FACE].astype(jnp.bfloat16)
    x_terms = jnp.dot(jnp.concatenate([high_1, low_1], -1), x_lift, preferred_element_type=jnp.float32)
    first = fixed + scale * (own + x_terms)
    below_plane = from_below[:, FACE:] + scale * jnp.dot(
        jnp.concatenate([high_2, low], -1), x_lift[:, high_cols], preferred_element_type=jnp.float32
    )
    above_plane = from_above[:, FACE:] + scale * jnp.dot(
        jnp.concatenate([high, low_2], -1), x_lift[:, low_cols], preferred_element_type=jnp.float32
    )
    own_1, _ = local_terms(first, reaction, weights, ny, nz)
    faces_1 = jnp.concatenate([below_plane.astype(jnp.bfloat16), above_plane.astype(jnp.bfloat16)], -1)
    applied = own_1 + jnp.dot(faces_1, x_lift, preferred_element_type=jnp.float32)
    if last_is_slope:
        return applied
    return fixed + scale * applied

def gather_nodes(rows):
    nodes = lax.axis_size("node")
    me = lax.axis_index("node")
    shifted = [rows] + [passed_along(rows, "node", shift) for shift in range(1, nodes)]
    return shifted, (me - jnp.arange(nodes)) % nodes


def local(start_state, node_states, reaction_rates, volume, face_lift):
    node_times, weights_table = quadrature_table(M)
    shape = node_states.shape
    ny, nz, points = shape[-3], shape[-2], shape[-1]
    rows = ny * nz
    local_count = shape[0]
    first_node = lax.axis_index("node") * local_count
    all_weights = jnp.asarray(weights_table, jnp.float32)
    own_weights = lax.dynamic_slice_in_dim(all_weights, first_node, local_count, 0)
    all_scales = jnp.asarray(time_step * node_times, jnp.float32)
    own_scale = lax.dynamic_slice_in_dim(all_scales, first_node, local_count, 0)[0]

    weights = spread_weights(volume, face_lift)
    x_lift = face_lift[: 2 * FACE]
    start = start_state.reshape((rows, points))
    reaction = reaction_rates.reshape((rows, points))
    states = node_states.reshape((rows, points))
    own_row = lax.dynamic_slice_in_dim(all_weights, first_node, 1, 0)[0]
    slopes = apply_operator(states, reaction, weights, x_lift, ny, nz)
    for sweep_index in range(SWEEPS):
        slope_rows = slopes.astype(jnp.bfloat16)
        received, sources = gather_nodes(slope_rows)
        source_weights = jnp.take(own_row, sources)
        stacked = jnp.stack(received).astype(jnp.float32)
        running_sum = jnp.sum(source_weights[:, None, None] * stacked, axis=0)
        fixed_part = start + time_step * running_sum - own_scale * slopes
        iterate = start + time_step * running_sum
        steps = INNER - 1 + (1 if sweep_index + 1 < SWEEPS else 0)
        if steps % 2:
            iterate = fixed_part + own_scale * apply_operator(iterate, reaction, weights, x_lift, ny, nz)
            steps -= 1
        for pair in range(steps // 2):
            last = sweep_index + 1 < SWEEPS and pair == steps // 2 - 1
            iterate = two_steps(iterate, fixed_part, own_scale, reaction, weights, x_lift, ny, nz, last)
        if sweep_index + 1 < SWEEPS:
            slopes = iterate
        else:
            states = iterate
    return states.reshape(shape)


def solution(mesh):
    in_specs = (
        P("gx", None, None, None),
        P("node", "gx", None, None, None),
        P("gx", None, None, None),
        P(),
        P(),
    )
    out_specs = P("node", "gx", None, None, None)
    return jax.shard_map(local, mesh=mesh, in_specs=in_specs, out_specs=out_specs, check_vma=False)
```

```python
import math

import jax
import jax.numpy as jnp
import numpy as np
from jax import lax
from jax.sharding import PartitionSpec as P

M = 8
NP = 8
SWEEPS = 2
INNER = 7
FACE = NP * NP


time_step = 0.45


def passed_along(array, axis, by):
    devices = lax.axis_size(axis)
    return lax.ppermute(array, axis, [(i, (i + by) % devices) for i in range(devices)])


def quadrature_table(node_count):
    roots_list = []
    for index in range(node_count):
        estimate = math.cos(math.pi * (index + 0.75) / (node_count + 0.5))
        for newton_step in range(60):
            previous, current = (1.0, estimate)
            for degree in range(2, node_count + 1):
                previous, current = (
                    current,
                    ((2 * degree - 1) * estimate * current - (degree - 1) * previous) / degree,
                )
            slope_value = node_count * (estimate * current - previous) / (estimate * estimate - 1.0)
            estimate = estimate - current / slope_value
        roots_list.append(0.5 * (estimate + 1.0))
    times_list = sorted(roots_list)
    weights_table = np.zeros((node_count, node_count))
    for column in range(node_count):
        coeffs = [1.0]
        scaling = 1.0
        for other in range(node_count):
            if other != column:
                point = times_list[other]
                widened = [0.0] * (len(coeffs) + 1)
                for power, entry in enumerate(coeffs):
                    widened[power + 1] += entry
                    widened[power] -= point * entry
                coeffs = widened
                scaling = scaling * (times_list[column] - point)
        for row in range(node_count):
            upper = times_list[row]
            total = 0.0
            for power, entry in enumerate(coeffs):
                total += entry / scaling * upper ** (power + 1) / (power + 1)
            weights_table[row, column] = total
    return (np.array(times_list), weights_table)


def face_selector(axis, value):
    a, b, c = np.meshgrid(np.arange(NP), np.arange(NP), np.arange(NP), indexing="ij")
    point = ((a * NP + b) * NP + c).reshape(-1)
    keep = [a, b, c][axis].reshape(-1) == value
    select = np.zeros((NP**3, FACE), np.float32)
    select[point[keep], np.arange(FACE)] = 1.0
    return select


def spread_weights(volume, face_lift):
    blocks = [volume]
    for index, (axis, value) in enumerate([(1, NP - 1), (1, 0), (2, NP - 1), (2, 0)]):
        rows = face_lift[(2 + index) * FACE : (3 + index) * FACE]
        select = jnp.asarray(face_selector(axis, value), jnp.bfloat16)
        blocks.append(jnp.dot(select, rows, preferred_element_type=jnp.float32).astype(jnp.bfloat16))
    return jnp.concatenate(blocks, axis=0)


def shifted_inputs(rounded, ny, nz):
    cube = rounded.reshape((ny, nz, -1))
    parts = [
        cube,
        jnp.roll(cube, 1, axis=0),
        jnp.roll(cube, -1, axis=0),
        jnp.roll(cube, 1, axis=1),
        jnp.roll(cube, -1, axis=1),
    ]
    return jnp.concatenate(parts, axis=-1).reshape((ny * nz, -1))


def local_terms(field, reaction, weights, ny, nz):
    rounded = field.astype(jnp.bfloat16)
    stacked = shifted_inputs(rounded, ny, nz)
    own = jnp.dot(stacked, weights, preferred_element_type=jnp.float32) - reaction * field
    return own, rounded


def swapped(array, axis, partner):
    devices = lax.axis_size(axis)
    return lax.ppermute(array, axis, [(i, partner(i) % devices) for i in range(devices)])


def exchange_faces(rounded):
    high = rounded[:, (NP - 1) * FACE :]
    low = rounded[:, :FACE]
    odd = lax.axis_index("gx") % 2 == 1
    first = swapped(jnp.where(odd, low, high), "gx", lambda i: i ^ 1)
    second = swapped(jnp.where(odd, high, low), "gx", lambda i: i + 1 if i % 2 else i - 1)
    below = jnp.where(odd, first, second)
    above = jnp.where(odd, second, first)
    return jnp.concatenate([below, above], axis=-1)


def apply_operator(field, reaction, weights, x_lift, ny, nz):
    own, rounded = local_terms(field, reaction, weights, ny, nz)
    faces = exchange_faces(rounded)
    return own + jnp.dot(faces, x_lift, preferred_element_type=jnp.float32)


def gather_nodes(rows):
    nodes = lax.axis_size("node")
    me = lax.axis_index("node")
    swaps = [rows] + [swapped(rows, "node", lambda i, k=k: i ^ k) for k in range(1, nodes)]
    return swaps, me ^ jnp.arange(nodes)


def local(start_state, node_states, reaction_rates, volume, face_lift):
    node_times, weights_table = quadrature_table(M)
    shape = node_states.shape
    ny, nz, points = shape[-3], shape[-2], shape[-1]
    rows = ny * nz
    local_count = shape[0]
    first_node = lax.axis_index("node") * local_count
    all_weights = jnp.asarray(weights_table, jnp.float32)
    own_weights = lax.dynamic_slice_in_dim(all_weights, first_node, local_count, 0)
    all_scales = jnp.asarray(time_step * node_times, jnp.float32)
    own_scale = lax.dynamic_slice_in_dim(all_scales, first_node, local_count, 0)[0]

    weights = spread_weights(volume, face_lift)
    x_lift = face_lift[: 2 * FACE]
    start = start_state.reshape((rows, points))
    reaction = reaction_rates.reshape((rows, points))
    states = node_states.reshape((rows, points))
    for sweep_index in range(SWEEPS):
        slopes = apply_operator(states, reaction, weights, x_lift, ny, nz)
        slope_rows = slopes.astype(jnp.bfloat16)
        received, sources = gather_nodes(slope_rows)
        source_weights = jnp.take(own_weights[0], sources)
        stacked = jnp.stack(received).astype(jnp.float32)
        running_sum = jnp.sum(source_weights[:, None, None] * stacked, axis=0)
        fixed_part = start + time_step * running_sum - own_scale * slopes
        iterate = start + time_step * running_sum
        for inner_step in range(INNER - 1):
            iterate = fixed_part + own_scale * apply_operator(iterate, reaction, weights, x_lift, ny, nz)
        states = iterate
    return states.reshape(shape)


def solution(mesh):
    in_specs = (
        P("gx", None, None, None),
        P("node", "gx", None, None, None),
        P("gx", None, None, None),
        P(),
        P(),
    )
    out_specs = P("node", "gx", None, None, None)
    return jax.shard_map(local, mesh=mesh, in_specs=in_specs, out_specs=out_specs, check_vma=False)
```

```python
import math

import jax
import jax.numpy as jnp
import numpy as np
from jax import lax
from jax.sharding import PartitionSpec as P

M = 8
NP = 8
SWEEPS = 2
INNER = 7
FACE = NP * NP


time_step = 0.45


def passed_along(array, axis, by):
    devices = lax.axis_size(axis)
    return lax.ppermute(array, axis, [(i, (i + by) % devices) for i in range(devices)])


def quadrature_table(node_count):
    roots_list = []
    for index in range(node_count):
        estimate = math.cos(math.pi * (index + 0.75) / (node_count + 0.5))
        for newton_step in range(60):
            previous, current = (1.0, estimate)
            for degree in range(2, node_count + 1):
                previous, current = (
                    current,
                    ((2 * degree - 1) * estimate * current - (degree - 1) * previous) / degree,
                )
            slope_value = node_count * (estimate * current - previous) / (estimate * estimate - 1.0)
            estimate = estimate - current / slope_value
        roots_list.append(0.5 * (estimate + 1.0))
    times_list = sorted(roots_list)
    weights_table = np.zeros((node_count, node_count))
    for column in range(node_count):
        coeffs = [1.0]
        scaling = 1.0
        for other in range(node_count):
            if other != column:
                point = times_list[other]
                widened = [0.0] * (len(coeffs) + 1)
                for power, entry in enumerate(coeffs):
                    widened[power + 1] += entry
                    widened[power] -= point * entry
                coeffs = widened
                scaling = scaling * (times_list[column] - point)
        for row in range(node_count):
            upper = times_list[row]
            total = 0.0
            for power, entry in enumerate(coeffs):
                total += entry / scaling * upper ** (power + 1) / (power + 1)
            weights_table[row, column] = total
    return (np.array(times_list), weights_table)


def face_selector(axis, value):
    a, b, c = np.meshgrid(np.arange(NP), np.arange(NP), np.arange(NP), indexing="ij")
    point = ((a * NP + b) * NP + c).reshape(-1)
    keep = [a, b, c][axis].reshape(-1) == value
    select = np.zeros((NP**3, FACE), np.float32)
    select[point[keep], np.arange(FACE)] = 1.0
    return select


def spread_weights(volume, face_lift):
    blocks = [volume]
    for index, (axis, value) in enumerate([(1, NP - 1), (1, 0), (2, NP - 1), (2, 0)]):
        rows = face_lift[(2 + index) * FACE : (3 + index) * FACE]
        select = jnp.asarray(face_selector(axis, value), jnp.bfloat16)
        blocks.append(jnp.dot(select, rows, preferred_element_type=jnp.float32).astype(jnp.bfloat16))
    return jnp.concatenate(blocks, axis=0)


def shifted_inputs(rounded, ny, nz):
    cube = rounded.reshape((ny, nz, -1))
    parts = [
        cube,
        jnp.roll(cube, 1, axis=0),
        jnp.roll(cube, -1, axis=0),
        jnp.roll(cube, 1, axis=1),
        jnp.roll(cube, -1, axis=1),
    ]
    return jnp.concatenate(parts, axis=-1).reshape((ny * nz, -1))


def local_terms(field, reaction, weights, ny, nz):
    rounded = field.astype(jnp.bfloat16)
    stacked = shifted_inputs(rounded, ny, nz)
    own = jnp.dot(stacked, weights, preferred_element_type=jnp.float32) - reaction * field
    return own, rounded


def swapped(array, axis, partner):
    devices = lax.axis_size(axis)
    return lax.ppermute(array, axis, [(i, partner(i) % devices) for i in range(devices)])


def exchange_faces(rounded):
    high = rounded[:, (NP - 1) * FACE :]
    low = rounded[:, :FACE]
    odd = lax.axis_index("gx") % 2 == 1
    first = swapped(jnp.where(odd, low, high), "gx", lambda i: i ^ 1)
    second = swapped(jnp.where(odd, high, low), "gx", lambda i: i + 1 if i % 2 else i - 1)
    below = jnp.where(odd, first, second)
    above = jnp.where(odd, second, first)
    return jnp.concatenate([below, above], axis=-1)


def apply_operator(field, reaction, weights, x_lift, ny, nz):
    own, rounded = local_terms(field, reaction, weights, ny, nz)
    faces = exchange_faces(rounded)
    return own + jnp.dot(faces, x_lift, preferred_element_type=jnp.float32)


def gather_nodes(rows):
    nodes = lax.axis_size("node")
    me = lax.axis_index("node")
    swaps = [rows] + [swapped(rows, "node", lambda i, k=k: i ^ k) for k in range(1, nodes)]
    return swaps, me ^ jnp.arange(nodes)


def local(start_state, node_states, reaction_rates, volume, face_lift):
    node_times, weights_table = quadrature_table(M)
    shape = node_states.shape
    ny, nz, points = shape[-3], shape[-2], shape[-1]
    rows = ny * nz
    local_count = shape[0]
    first_node = lax.axis_index("node") * local_count
    all_weights = jnp.asarray(weights_table, jnp.float32)
    own_weights = lax.dynamic_slice_in_dim(all_weights, first_node, local_count, 0)
    all_scales = jnp.asarray(time_step * node_times, jnp.float32)
    own_scale = lax.dynamic_slice_in_dim(all_scales, first_node, local_count, 0)[0]

    weights = spread_weights(volume, face_lift)
    x_lift = face_lift[: 2 * FACE]
    start = start_state.reshape((rows, points))
    reaction = reaction_rates.reshape((rows, points))
    states = node_states.reshape((rows, points))
    for sweep_index in range(SWEEPS):
        slopes = apply_operator(states, reaction, weights, x_lift, ny, nz)
        slope_rows = slopes.astype(jnp.bfloat16)
        received, sources = gather_nodes(slope_rows)
        source_weights = jnp.take(own_weights[0], sources)
        stacked = jnp.stack(received).astype(jnp.float32)
        running_sum = jnp.sum(source_weights[:, None, None] * stacked, axis=0)
        fixed_part = start + time_step * running_sum - own_scale * slopes
        iterate = start + time_step * running_sum
        def inner(step, value):
            return fixed_part + own_scale * apply_operator(value, reaction, weights, x_lift, ny, nz)

        iterate = lax.fori_loop(0, INNER - 1, inner, iterate)
        states = iterate
    return states.reshape(shape)


def solution(mesh):
    in_specs = (
        P("gx", None, None, None),
        P("node", "gx", None, None, None),
        P("gx", None, None, None),
        P(),
        P(),
    )
    out_specs = P("node", "gx", None, None, None)
    return jax.shard_map(local, mesh=mesh, in_specs=in_specs, out_specs=out_specs, check_vma=False)
```

```python
import math

import jax
import jax.numpy as jnp
import numpy as np
from jax import lax
from jax.sharding import PartitionSpec as P

M = 8
NP = 8
SWEEPS = 2
INNER = 7
FACE = NP * NP


time_step = 0.45


def passed_along(array, axis, by):
    devices = lax.axis_size(axis)
    return lax.ppermute(array, axis, [(i, (i + by) % devices) for i in range(devices)])


def quadrature_table(node_count):
    roots_list = []
    for index in range(node_count):
        estimate = math.cos(math.pi * (index + 0.75) / (node_count + 0.5))
        for newton_step in range(60):
            previous, current = (1.0, estimate)
            for degree in range(2, node_count + 1):
                previous, current = (
                    current,
                    ((2 * degree - 1) * estimate * current - (degree - 1) * previous) / degree,
                )
            slope_value = node_count * (estimate * current - previous) / (estimate * estimate - 1.0)
            estimate = estimate - current / slope_value
        roots_list.append(0.5 * (estimate + 1.0))
    times_list = sorted(roots_list)
    weights_table = np.zeros((node_count, node_count))
    for column in range(node_count):
        coeffs = [1.0]
        scaling = 1.0
        for other in range(node_count):
            if other != column:
                point = times_list[other]
                widened = [0.0] * (len(coeffs) + 1)
                for power, entry in enumerate(coeffs):
                    widened[power + 1] += entry
                    widened[power] -= point * entry
                coeffs = widened
                scaling = scaling * (times_list[column] - point)
        for row in range(node_count):
            upper = times_list[row]
            total = 0.0
            for power, entry in enumerate(coeffs):
                total += entry / scaling * upper ** (power + 1) / (power + 1)
            weights_table[row, column] = total
    return (np.array(times_list), weights_table)


def face_selector(axis, value):
    a, b, c = np.meshgrid(np.arange(NP), np.arange(NP), np.arange(NP), indexing="ij")
    point = ((a * NP + b) * NP + c).reshape(-1)
    keep = [a, b, c][axis].reshape(-1) == value
    select = np.zeros((NP**3, FACE), np.float32)
    select[point[keep], np.arange(FACE)] = 1.0
    return select


def spread_weights(volume, face_lift):
    blocks = [volume]
    for index, (axis, value) in enumerate([(1, NP - 1), (1, 0), (2, NP - 1), (2, 0)]):
        rows = face_lift[(2 + index) * FACE : (3 + index) * FACE]
        select = jnp.asarray(face_selector(axis, value), jnp.bfloat16)
        blocks.append(jnp.dot(select, rows, preferred_element_type=jnp.float32).astype(jnp.bfloat16))
    return jnp.concatenate(blocks, axis=0)


def shifted_inputs(rounded, ny, nz):
    cube = rounded.reshape((ny, nz, -1))
    parts = [
        cube,
        jnp.roll(cube, 1, axis=0),
        jnp.roll(cube, -1, axis=0),
        jnp.roll(cube, 1, axis=1),
        jnp.roll(cube, -1, axis=1),
    ]
    return jnp.concatenate(parts, axis=-1).reshape((ny * nz, -1))


def local_terms(field, reaction, weights, ny, nz):
    rounded = field.astype(jnp.bfloat16)
    stacked = shifted_inputs(rounded, ny, nz)
    own = jnp.dot(stacked, weights, preferred_element_type=jnp.float32) - reaction * field
    return own, rounded


def swapped(array, axis, partner):
    devices = lax.axis_size(axis)
    return lax.ppermute(array, axis, [(i, partner(i) % devices) for i in range(devices)])


def exchange_faces(rounded):
    high = rounded[:, (NP - 1) * FACE :]
    low = rounded[:, :FACE]
    odd = lax.axis_index("gx") % 2 == 1
    first = swapped(jnp.where(odd, low, high), "gx", lambda i: i ^ 1)
    second = swapped(jnp.where(odd, high, low), "gx", lambda i: i + 1 if i % 2 else i - 1)
    below = jnp.where(odd, first, second)
    above = jnp.where(odd, second, first)
    return jnp.concatenate([below, above], axis=-1)


def apply_operator(field, reaction, weights, x_lift, ny, nz):
    own, rounded = local_terms(field, reaction, weights, ny, nz)
    faces = exchange_faces(rounded)
    return own + jnp.dot(faces, x_lift, preferred_element_type=jnp.float32)


def two_steps(field, fixed, scale, reaction, weights, x_lift, ny, nz, last_is_slope):
    high_cols = slice((NP - 1) * FACE, NP * FACE)
    low_cols = slice(0, FACE)
    odd = lax.axis_index("gx") % 2 == 1
    on_chip = lambda i: i ^ 1
    far = lambda i: i + 1 if i % 2 else i - 1
    rounded = field.astype(jnp.bfloat16)
    high = rounded[:, high_cols]
    low = rounded[:, low_cols]
    chip_faces = swapped(jnp.where(odd, low, high), "gx", on_chip)
    own, _ = local_terms(field, reaction, weights, ny, nz)
    part_high = fixed[:, high_cols] + scale * own[:, high_cols]
    part_low = fixed[:, low_cols] + scale * own[:, low_cols]
    far_send = jnp.where(
        odd,
        jnp.concatenate([high.astype(jnp.float32), part_high, chip_faces.astype(jnp.float32)], -1),
        jnp.concatenate([low.astype(jnp.float32), part_low, chip_faces.astype(jnp.float32)], -1),
    )
    far_got = swapped(far_send, "gx", far)
    far_face = far_got[:, :FACE]
    far_part = far_got[:, FACE : 2 * FACE]
    far_second = far_got[:, 2 * FACE :].astype(jnp.bfloat16)
    chip_send = jnp.where(
        odd,
        jnp.concatenate([part_low, far_face], -1),
        jnp.concatenate([part_high, far_face], -1),
    )
    chip_got = swapped(chip_send, "gx", on_chip)
    chip_part = chip_got[:, :FACE]
    chip_second = chip_got[:, FACE:].astype(jnp.bfloat16)
    far_face = far_face.astype(jnp.bfloat16)
    below_1 = jnp.where(odd, chip_faces, far_face)
    above_1 = jnp.where(odd, far_face, chip_faces)
    below_part = jnp.where(odd, chip_part, far_part)
    above_part = jnp.where(odd, far_part, chip_part)
    below_2 = jnp.where(odd, chip_second, far_second)
    above_2 = jnp.where(odd, far_second, chip_second)
    x_terms = jnp.dot(jnp.concatenate([below_1, above_1], -1), x_lift, preferred_element_type=jnp.float32)
    first = fixed + scale * (own + x_terms)
    below_plane = below_part + scale * jnp.dot(
        jnp.concatenate([below_2, low], -1), x_lift[:, high_cols], preferred_element_type=jnp.float32
    )
    above_plane = above_part + scale * jnp.dot(
        jnp.concatenate([high, above_2], -1), x_lift[:, low_cols], preferred_element_type=jnp.float32
    )
    own_1, _ = local_terms(first, reaction, weights, ny, nz)
    faces_1 = jnp.concatenate([below_plane.astype(jnp.bfloat16), above_plane.astype(jnp.bfloat16)], -1)
    applied = own_1 + jnp.dot(faces_1, x_lift, preferred_element_type=jnp.float32)
    if last_is_slope:
        return applied
    return fixed + scale * applied


def gather_nodes(rows):
    nodes = lax.axis_size("node")
    me = lax.axis_index("node")
    swaps = [rows] + [swapped(rows, "node", lambda i, k=k: i ^ k) for k in range(1, nodes)]
    return swaps, me ^ jnp.arange(nodes)


def local(start_state, node_states, reaction_rates, volume, face_lift):
    node_times, weights_table = quadrature_table(M)
    shape = node_states.shape
    ny, nz, points = shape[-3], shape[-2], shape[-1]
    rows = ny * nz
    local_count = shape[0]
    first_node = lax.axis_index("node") * local_count
    all_weights = jnp.asarray(weights_table, jnp.float32)
    own_weights = lax.dynamic_slice_in_dim(all_weights, first_node, local_count, 0)
    all_scales = jnp.asarray(time_step * node_times, jnp.float32)
    own_scale = lax.dynamic_slice_in_dim(all_scales, first_node, local_count, 0)[0]

    weights = spread_weights(volume, face_lift)
    x_lift = face_lift[: 2 * FACE]
    start = start_state.reshape((rows, points))
    reaction = reaction_rates.reshape((rows, points))
    states = node_states.reshape((rows, points))
    slopes = apply_operator(states, reaction, weights, x_lift, ny, nz)
    for sweep_index in range(SWEEPS):
        slope_rows = slopes.astype(jnp.bfloat16)
        received, sources = gather_nodes(slope_rows)
        source_weights = jnp.take(own_weights[0], sources)
        stacked = jnp.stack(received).astype(jnp.float32)
        running_sum = jnp.sum(source_weights[:, None, None] * stacked, axis=0)
        fixed_part = start + time_step * running_sum - own_scale * slopes
        iterate = start + time_step * running_sum
        more = sweep_index + 1 < SWEEPS
        steps = INNER - 1 + (1 if more else 0)
        if steps % 2:
            iterate = fixed_part + own_scale * apply_operator(iterate, reaction, weights, x_lift, ny, nz)
            steps -= 1
        for pair in range(steps // 2):
            last = more and pair == steps // 2 - 1
            iterate = two_steps(iterate, fixed_part, own_scale, reaction, weights, x_lift, ny, nz, last)
        if more:
            slopes = iterate
        else:
            states = iterate
    return states.reshape(shape)


def solution(mesh):
    in_specs = (
        P("gx", None, None, None),
        P("node", "gx", None, None, None),
        P("gx", None, None, None),
        P(),
        P(),
    )
    out_specs = P("node", "gx", None, None, None)
    return jax.shard_map(local, mesh=mesh, in_specs=in_specs, out_specs=out_specs, check_vma=False)
```

```python
import math

import jax
import jax.numpy as jnp
import numpy as np
from jax import lax
from jax.sharding import PartitionSpec as P

M = 8
NP = 8
SWEEPS = 2
INNER = 7
FACE = NP * NP


time_step = 0.45


def passed_along(array, axis, by):
    devices = lax.axis_size(axis)
    return lax.ppermute(array, axis, [(i, (i + by) % devices) for i in range(devices)])


def quadrature_table(node_count):
    roots_list = []
    for index in range(node_count):
        estimate = math.cos(math.pi * (index + 0.75) / (node_count + 0.5))
        for newton_step in range(60):
            previous, current = (1.0, estimate)
            for degree in range(2, node_count + 1):
                previous, current = (
                    current,
                    ((2 * degree - 1) * estimate * current - (degree - 1) * previous) / degree,
                )
            slope_value = node_count * (estimate * current - previous) / (estimate * estimate - 1.0)
            estimate = estimate - current / slope_value
        roots_list.append(0.5 * (estimate + 1.0))
    times_list = sorted(roots_list)
    weights_table = np.zeros((node_count, node_count))
    for column in range(node_count):
        coeffs = [1.0]
        scaling = 1.0
        for other in range(node_count):
            if other != column:
                point = times_list[other]
                widened = [0.0] * (len(coeffs) + 1)
                for power, entry in enumerate(coeffs):
                    widened[power + 1] += entry
                    widened[power] -= point * entry
                coeffs = widened
                scaling = scaling * (times_list[column] - point)
        for row in range(node_count):
            upper = times_list[row]
            total = 0.0
            for power, entry in enumerate(coeffs):
                total += entry / scaling * upper ** (power + 1) / (power + 1)
            weights_table[row, column] = total
    return (np.array(times_list), weights_table)


def face_selector(axis, value):
    a, b, c = np.meshgrid(np.arange(NP), np.arange(NP), np.arange(NP), indexing="ij")
    point = ((a * NP + b) * NP + c).reshape(-1)
    keep = [a, b, c][axis].reshape(-1) == value
    select = np.zeros((NP**3, FACE), np.float32)
    select[point[keep], np.arange(FACE)] = 1.0
    return select


def face_weights(volume, face_lift):
    select = np.concatenate(
        [face_selector(axis, value) for axis, value in [(1, NP - 1), (1, 0), (2, NP - 1), (2, 0)]], axis=1
    )
    stacked = jnp.concatenate([volume, face_lift[2 * FACE :]], axis=0)
    return jnp.asarray(select, jnp.bfloat16), stacked


def local_terms(field, reaction, weights, ny, nz):
    select, stacked = weights
    rounded = field.astype(jnp.bfloat16)
    faces = jnp.dot(rounded, select, preferred_element_type=jnp.float32).astype(jnp.bfloat16)
    cube = faces.reshape((ny, nz, 4, FACE))
    moved = jnp.concatenate(
        [
            jnp.roll(cube[:, :, 0], 1, axis=0),
            jnp.roll(cube[:, :, 1], -1, axis=0),
            jnp.roll(cube[:, :, 2], 1, axis=1),
            jnp.roll(cube[:, :, 3], -1, axis=1),
        ],
        axis=-1,
    ).reshape((ny * nz, 4 * FACE))
    inputs = jnp.concatenate([rounded, moved], axis=-1)
    own = jnp.dot(inputs, stacked, preferred_element_type=jnp.float32) - reaction * field
    return own, rounded


def swapped(array, axis, partner):
    devices = lax.axis_size(axis)
    return lax.ppermute(array, axis, [(i, partner(i) % devices) for i in range(devices)])


def exchange_faces(rounded):
    high = rounded[:, (NP - 1) * FACE :]
    low = rounded[:, :FACE]
    odd = lax.axis_index("gx") % 2 == 1
    first = swapped(jnp.where(odd, low, high), "gx", lambda i: i ^ 1)
    second = swapped(jnp.where(odd, high, low), "gx", lambda i: i + 1 if i % 2 else i - 1)
    below = jnp.where(odd, first, second)
    above = jnp.where(odd, second, first)
    return jnp.concatenate([below, above], axis=-1)


def apply_operator(field, reaction, weights, x_lift, ny, nz):
    own, rounded = local_terms(field, reaction, weights, ny, nz)
    faces = exchange_faces(rounded)
    return own + jnp.dot(faces, x_lift, preferred_element_type=jnp.float32)


def gather_nodes(rows):
    nodes = lax.axis_size("node")
    me = lax.axis_index("node")
    swaps = [rows] + [swapped(rows, "node", lambda i, k=k: i ^ k) for k in range(1, nodes)]
    return swaps, me ^ jnp.arange(nodes)


def local(start_state, node_states, reaction_rates, volume, face_lift):
    node_times, weights_table = quadrature_table(M)
    shape = node_states.shape
    ny, nz, points = shape[-3], shape[-2], shape[-1]
    rows = ny * nz
    local_count = shape[0]
    first_node = lax.axis_index("node") * local_count
    all_weights = jnp.asarray(weights_table, jnp.float32)
    own_weights = lax.dynamic_slice_in_dim(all_weights, first_node, local_count, 0)
    all_scales = jnp.asarray(time_step * node_times, jnp.float32)
    own_scale = lax.dynamic_slice_in_dim(all_scales, first_node, local_count, 0)[0]

    weights = face_weights(volume, face_lift)
    x_lift = face_lift[: 2 * FACE]
    start = start_state.reshape((rows, points))
    reaction = reaction_rates.reshape((rows, points))
    states = node_states.reshape((rows, points))
    for sweep_index in range(SWEEPS):
        slopes = apply_operator(states, reaction, weights, x_lift, ny, nz)
        slope_rows = slopes.astype(jnp.bfloat16)
        received, sources = gather_nodes(slope_rows)
        source_weights = jnp.take(own_weights[0], sources)
        stacked = jnp.stack(received).astype(jnp.float32)
        running_sum = jnp.sum(source_weights[:, None, None] * stacked, axis=0)
        fixed_part = start + time_step * running_sum - own_scale * slopes
        iterate = start + time_step * running_sum
        for inner_step in range(INNER - 1):
            iterate = fixed_part + own_scale * apply_operator(iterate, reaction, weights, x_lift, ny, nz)
        states = iterate
    return states.reshape(shape)


def solution(mesh):
    in_specs = (
        P("gx", None, None, None),
        P("node", "gx", None, None, None),
        P("gx", None, None, None),
        P(),
        P(),
    )
    out_specs = P("node", "gx", None, None, None)
    return jax.shard_map(local, mesh=mesh, in_specs=in_specs, out_specs=out_specs, check_vma=False)
```

```python
import math

import jax
import jax.numpy as jnp
import numpy as np
from jax import lax
from jax.sharding import PartitionSpec as P

M = 8
NP = 8
SWEEPS = 2
INNER = 7
FACE = NP * NP


time_step = 0.45


def passed_along(array, axis, by):
    devices = lax.axis_size(axis)
    return lax.ppermute(array, axis, [(i, (i + by) % devices) for i in range(devices)])


def quadrature_table(node_count):
    roots_list = []
    for index in range(node_count):
        estimate = math.cos(math.pi * (index + 0.75) / (node_count + 0.5))
        for newton_step in range(60):
            previous, current = (1.0, estimate)
            for degree in range(2, node_count + 1):
                previous, current = (
                    current,
                    ((2 * degree - 1) * estimate * current - (degree - 1) * previous) / degree,
                )
            slope_value = node_count * (estimate * current - previous) / (estimate * estimate - 1.0)
            estimate = estimate - current / slope_value
        roots_list.append(0.5 * (estimate + 1.0))
    times_list = sorted(roots_list)
    weights_table = np.zeros((node_count, node_count))
    for column in range(node_count):
        coeffs = [1.0]
        scaling = 1.0
        for other in range(node_count):
            if other != column:
                point = times_list[other]
                widened = [0.0] * (len(coeffs) + 1)
                for power, entry in enumerate(coeffs):
                    widened[power + 1] += entry
                    widened[power] -= point * entry
                coeffs = widened
                scaling = scaling * (times_list[column] - point)
        for row in range(node_count):
            upper = times_list[row]
            total = 0.0
            for power, entry in enumerate(coeffs):
                total += entry / scaling * upper ** (power + 1) / (power + 1)
            weights_table[row, column] = total
    return (np.array(times_list), weights_table)


def face_selector(axis, value):
    a, b, c = np.meshgrid(np.arange(NP), np.arange(NP), np.arange(NP), indexing="ij")
    point = ((a * NP + b) * NP + c).reshape(-1)
    keep = [a, b, c][axis].reshape(-1) == value
    select = np.zeros((NP**3, FACE), np.float32)
    select[point[keep], np.arange(FACE)] = 1.0
    return select


def face_weights(volume, face_lift):
    picks = np.concatenate(
        [face_selector(axis, value) for axis, value in [(1, NP - 1), (1, 0), (2, NP - 1), (2, 0)]], axis=1
    ).argmax(axis=0)
    rows = lax.broadcasted_iota(jnp.int32, (NP**3, 4 * FACE), 0)
    select = (rows == jnp.asarray(picks, jnp.int32)[None, :]).astype(jnp.bfloat16)
    stacked = jnp.concatenate([volume, face_lift[2 * FACE :]], axis=0)
    return select, stacked


def local_terms(field, reaction, weights, ny, nz):
    select, stacked = weights
    rounded = field.astype(jnp.bfloat16)
    faces = jnp.dot(rounded, select, preferred_element_type=jnp.float32).astype(jnp.bfloat16)
    cube = faces.reshape((ny, nz, 4, FACE))
    moved = jnp.concatenate(
        [
            jnp.roll(cube[:, :, 0], 1, axis=0),
            jnp.roll(cube[:, :, 1], -1, axis=0),
            jnp.roll(cube[:, :, 2], 1, axis=1),
            jnp.roll(cube[:, :, 3], -1, axis=1),
        ],
        axis=-1,
    ).reshape((ny * nz, 4 * FACE))
    inputs = jnp.concatenate([rounded, moved], axis=-1)
    own = jnp.dot(inputs, stacked, preferred_element_type=jnp.float32) - reaction * field
    return own, rounded


def swapped(array, axis, partner):
    devices = lax.axis_size(axis)
    return lax.ppermute(array, axis, [(i, partner(i) % devices) for i in range(devices)])


def exchange_faces(high, low):
    odd = lax.axis_index("gx") % 2 == 1
    first = swapped(jnp.where(odd, low, high), "gx", lambda i: i ^ 1)
    second = swapped(jnp.where(odd, high, low), "gx", lambda i: i + 1 if i % 2 else i - 1)
    below = jnp.where(odd, first, second)
    above = jnp.where(odd, second, first)
    return jnp.concatenate([below, above], axis=-1)


def face_planes(field):
    rounded = field.astype(jnp.bfloat16)
    return rounded[:, (NP - 1) * FACE :], rounded[:, :FACE]


def apply_operator(field, planes, reaction, weights, x_lift, ny, nz):
    faces = exchange_faces(*planes)
    own, _ = local_terms(field, reaction, weights, ny, nz)
    return own, jnp.dot(faces, x_lift, preferred_element_type=jnp.float32)


def step(field, planes, fixed, scale, reaction, weights, x_lift, ny, nz):
    own, x_terms = apply_operator(field, planes, reaction, weights, x_lift, ny, nz)
    edge = [slice((NP - 1) * FACE, NP * FACE), slice(0, FACE)]
    next_planes = tuple(
        (fixed[:, cols] + scale * (own[:, cols] + x_terms[:, cols])).astype(jnp.bfloat16) for cols in edge
    )
    next_planes = lax.optimization_barrier(next_planes)
    return fixed + scale * (own + x_terms), next_planes


def gather_nodes(rows):
    nodes = lax.axis_size("node")
    me = lax.axis_index("node")
    swaps = [rows] + [swapped(rows, "node", lambda i, k=k: i ^ k) for k in range(1, nodes)]
    return swaps, me ^ jnp.arange(nodes)


def local(start_state, node_states, reaction_rates, volume, face_lift):
    node_times, weights_table = quadrature_table(M)
    shape = node_states.shape
    ny, nz, points = shape[-3], shape[-2], shape[-1]
    rows = ny * nz
    local_count = shape[0]
    first_node = lax.axis_index("node") * local_count
    all_weights = jnp.asarray(weights_table, jnp.float32)
    own_weights = lax.dynamic_slice_in_dim(all_weights, first_node, local_count, 0)
    all_scales = jnp.asarray(time_step * node_times, jnp.float32)
    own_scale = lax.dynamic_slice_in_dim(all_scales, first_node, local_count, 0)[0]

    weights = face_weights(volume, face_lift)
    x_lift = face_lift[: 2 * FACE]
    start = start_state.reshape((rows, points))
    reaction = reaction_rates.reshape((rows, points))
    states = node_states.reshape((rows, points))
    for sweep_index in range(SWEEPS):
        own, x_terms = apply_operator(states, face_planes(states), reaction, weights, x_lift, ny, nz)
        slopes = own + x_terms
        slope_rows = slopes.astype(jnp.bfloat16)
        received, sources = gather_nodes(slope_rows)
        source_weights = jnp.take(own_weights[0], sources)
        stacked = jnp.stack(received).astype(jnp.float32)
        running_sum = jnp.sum(source_weights[:, None, None] * stacked, axis=0)
        fixed_part = start + time_step * running_sum - own_scale * slopes
        iterate = start + time_step * running_sum
        planes = face_planes(iterate)
        for inner_step in range(INNER - 1):
            iterate, planes = step(iterate, planes, fixed_part, own_scale, reaction, weights, x_lift, ny, nz)
        states = iterate
    return states.reshape(shape)


def solution(mesh):
    in_specs = (
        P("gx", None, None, None),
        P("node", "gx", None, None, None),
        P("gx", None, None, None),
        P(),
        P(),
    )
    out_specs = P("node", "gx", None, None, None)
    return jax.shard_map(local, mesh=mesh, in_specs=in_specs, out_specs=out_specs, check_vma=False)
```

```python
import math

import jax
import jax.numpy as jnp
import numpy as np
from jax import lax
from jax.sharding import PartitionSpec as P

M = 8
NP = 8
SWEEPS = 2
INNER = 7
FACE = NP * NP


time_step = 0.45


def passed_along(array, axis, by):
    devices = lax.axis_size(axis)
    return lax.ppermute(array, axis, [(i, (i + by) % devices) for i in range(devices)])


def quadrature_table(node_count):
    roots_list = []
    for index in range(node_count):
        estimate = math.cos(math.pi * (index + 0.75) / (node_count + 0.5))
        for newton_step in range(60):
            previous, current = (1.0, estimate)
            for degree in range(2, node_count + 1):
                previous, current = (
                    current,
                    ((2 * degree - 1) * estimate * current - (degree - 1) * previous) / degree,
                )
            slope_value = node_count * (estimate * current - previous) / (estimate * estimate - 1.0)
            estimate = estimate - current / slope_value
        roots_list.append(0.5 * (estimate + 1.0))
    times_list = sorted(roots_list)
    weights_table = np.zeros((node_count, node_count))
    for column in range(node_count):
        coeffs = [1.0]
        scaling = 1.0
        for other in range(node_count):
            if other != column:
                point = times_list[other]
                widened = [0.0] * (len(coeffs) + 1)
                for power, entry in enumerate(coeffs):
                    widened[power + 1] += entry
                    widened[power] -= point * entry
                coeffs = widened
                scaling = scaling * (times_list[column] - point)
        for row in range(node_count):
            upper = times_list[row]
            total = 0.0
            for power, entry in enumerate(coeffs):
                total += entry / scaling * upper ** (power + 1) / (power + 1)
            weights_table[row, column] = total
    return (np.array(times_list), weights_table)


def face_selector(axis, value):
    a, b, c = np.meshgrid(np.arange(NP), np.arange(NP), np.arange(NP), indexing="ij")
    point = ((a * NP + b) * NP + c).reshape(-1)
    keep = [a, b, c][axis].reshape(-1) == value
    select = np.zeros((NP**3, FACE), np.float32)
    select[point[keep], np.arange(FACE)] = 1.0
    return select


def face_weights(volume, face_lift):
    select = np.concatenate(
        [face_selector(axis, value) for axis, value in [(1, NP - 1), (1, 0), (2, NP - 1), (2, 0)]], axis=1
    )
    stacked = jnp.concatenate([volume, face_lift[2 * FACE :]], axis=0)
    return jnp.asarray(select, jnp.bfloat16), stacked


def local_terms(field, reaction, weights, ny, nz):
    select, stacked = weights
    rounded = field.astype(jnp.bfloat16)
    faces = jnp.dot(rounded, select, preferred_element_type=jnp.float32).astype(jnp.bfloat16)
    cube = faces.reshape((ny, nz, 4, FACE))
    moved = jnp.concatenate(
        [
            jnp.roll(cube[:, :, 0], 1, axis=0),
            jnp.roll(cube[:, :, 1], -1, axis=0),
            jnp.roll(cube[:, :, 2], 1, axis=1),
            jnp.roll(cube[:, :, 3], -1, axis=1),
        ],
        axis=-1,
    ).reshape((ny * nz, 4 * FACE))
    inputs = jnp.concatenate([rounded, moved], axis=-1)
    own = jnp.dot(inputs, stacked, preferred_element_type=jnp.float32) - reaction * field
    return own, rounded


def swapped(array, axis, partner):
    devices = lax.axis_size(axis)
    return lax.ppermute(array, axis, [(i, partner(i) % devices) for i in range(devices)])


def ring_order(devices):
    tops = devices // 4
    order = []
    for place in range(devices):
        half = devices // 2
        z = place // 2 if place < half else tops - 1 - (place - half) // 2
        order.append((z * 2 + (place >= half)) * 2 + place % 2)
    return order


def exchange_faces(rounded):
    high = rounded[:, (NP - 1) * FACE :]
    low = rounded[:, :FACE]
    devices = lax.axis_size("gx")
    order = ring_order(devices)
    place = {device: index for index, device in enumerate(order)}
    far = lambda i: order[(place[i] + 1 if place[i] % 2 else place[i] - 1) % devices]
    odd = lax.axis_index("gx") % 2 == 1
    first = swapped(jnp.where(odd, low, high), "gx", lambda i: i ^ 1)
    second = swapped(jnp.where(odd, high, low), "gx", far)
    below = jnp.where(odd, first, second)
    above = jnp.where(odd, second, first)
    return jnp.concatenate([below, above], axis=-1)


def to_ring(array):
    order = ring_order(lax.axis_size("gx"))
    return lax.ppermute(array, "gx", [(slab, device) for slab, device in enumerate(order)])


def from_ring(array):
    order = ring_order(lax.axis_size("gx"))
    return lax.ppermute(array, "gx", [(device, slab) for slab, device in enumerate(order)])


def apply_operator(field, reaction, weights, x_lift, ny, nz):
    own, rounded = local_terms(field, reaction, weights, ny, nz)
    faces = exchange_faces(rounded)
    return own + jnp.dot(faces, x_lift, preferred_element_type=jnp.float32)


def gather_nodes(rows):
    nodes = lax.axis_size("node")
    me = lax.axis_index("node")
    swaps = [rows] + [swapped(rows, "node", lambda i, k=k: i ^ k) for k in range(1, nodes)]
    return swaps, me ^ jnp.arange(nodes)


def local(start_state, node_states, reaction_rates, volume, face_lift):
    node_times, weights_table = quadrature_table(M)
    shape = node_states.shape
    ny, nz, points = shape[-3], shape[-2], shape[-1]
    rows = ny * nz
    local_count = shape[0]
    first_node = lax.axis_index("node") * local_count
    all_weights = jnp.asarray(weights_table, jnp.float32)
    own_weights = lax.dynamic_slice_in_dim(all_weights, first_node, local_count, 0)
    all_scales = jnp.asarray(time_step * node_times, jnp.float32)
    own_scale = lax.dynamic_slice_in_dim(all_scales, first_node, local_count, 0)[0]

    weights = face_weights(volume, face_lift)
    x_lift = face_lift[: 2 * FACE]
    moved = to_ring(
        jnp.concatenate([node_states.reshape((rows, points)), reaction_rates.reshape((rows, points))], -1)
    )
    states = moved[:, :points]
    reaction = moved[:, points:]
    start = to_ring(start_state.reshape((rows, points)))
    for sweep_index in range(SWEEPS):
        slopes = apply_operator(states, reaction, weights, x_lift, ny, nz)
        slope_rows = slopes.astype(jnp.bfloat16)
        received, sources = gather_nodes(slope_rows)
        source_weights = jnp.take(own_weights[0], sources)
        stacked = jnp.stack(received).astype(jnp.float32)
        running_sum = jnp.sum(source_weights[:, None, None] * stacked, axis=0)
        fixed_part = start + time_step * running_sum - own_scale * slopes
        iterate = start + time_step * running_sum
        for inner_step in range(INNER - 1):
            iterate = fixed_part + own_scale * apply_operator(iterate, reaction, weights, x_lift, ny, nz)
        states = iterate
    return from_ring(states).reshape(shape)


def solution(mesh):
    in_specs = (
        P("gx", None, None, None),
        P("node", "gx", None, None, None),
        P("gx", None, None, None),
        P(),
        P(),
    )
    out_specs = P("node", "gx", None, None, None)
    return jax.shard_map(local, mesh=mesh, in_specs=in_specs, out_specs=out_specs, check_vma=False)
```

```python
import math

import jax
import jax.numpy as jnp
import numpy as np
from jax import lax
from jax.sharding import PartitionSpec as P

M = 8
NP = 8
SWEEPS = 2
INNER = 7
FACE = NP * NP


time_step = 0.45


def passed_along(array, axis, by):
    devices = lax.axis_size(axis)
    return lax.ppermute(array, axis, [(i, (i + by) % devices) for i in range(devices)])


def quadrature_table(node_count):
    roots_list = []
    for index in range(node_count):
        estimate = math.cos(math.pi * (index + 0.75) / (node_count + 0.5))
        for newton_step in range(60):
            previous, current = (1.0, estimate)
            for degree in range(2, node_count + 1):
                previous, current = (
                    current,
                    ((2 * degree - 1) * estimate * current - (degree - 1) * previous) / degree,
                )
            slope_value = node_count * (estimate * current - previous) / (estimate * estimate - 1.0)
            estimate = estimate - current / slope_value
        roots_list.append(0.5 * (estimate + 1.0))
    times_list = sorted(roots_list)
    weights_table = np.zeros((node_count, node_count))
    for column in range(node_count):
        coeffs = [1.0]
        scaling = 1.0
        for other in range(node_count):
            if other != column:
                point = times_list[other]
                widened = [0.0] * (len(coeffs) + 1)
                for power, entry in enumerate(coeffs):
                    widened[power + 1] += entry
                    widened[power] -= point * entry
                coeffs = widened
                scaling = scaling * (times_list[column] - point)
        for row in range(node_count):
            upper = times_list[row]
            total = 0.0
            for power, entry in enumerate(coeffs):
                total += entry / scaling * upper ** (power + 1) / (power + 1)
            weights_table[row, column] = total
    return (np.array(times_list), weights_table)


def face_selector(axis, value):
    a, b, c = np.meshgrid(np.arange(NP), np.arange(NP), np.arange(NP), indexing="ij")
    point = ((a * NP + b) * NP + c).reshape(-1)
    keep = [a, b, c][axis].reshape(-1) == value
    select = np.zeros((NP**3, FACE), np.float32)
    select[point[keep], np.arange(FACE)] = 1.0
    return select


def face_weights(volume, face_lift):
    select = np.concatenate(
        [face_selector(axis, value) for axis, value in [(1, NP - 1), (1, 0), (2, NP - 1), (2, 0)]], axis=1
    )
    stacked = jnp.concatenate([volume, face_lift[2 * FACE :]], axis=0)
    return jnp.asarray(select, jnp.bfloat16), stacked


def local_terms(field, reaction, weights, ny, nz):
    select, stacked = weights
    rounded = field.astype(jnp.bfloat16)
    faces = jnp.dot(rounded, select, preferred_element_type=jnp.float32).astype(jnp.bfloat16)
    cube = faces.reshape((ny, nz, 4, FACE))
    moved = jnp.concatenate(
        [
            jnp.roll(cube[:, :, 0], 1, axis=0),
            jnp.roll(cube[:, :, 1], -1, axis=0),
            jnp.roll(cube[:, :, 2], 1, axis=1),
            jnp.roll(cube[:, :, 3], -1, axis=1),
        ],
        axis=-1,
    ).reshape((ny * nz, 4 * FACE))
    inputs = jnp.concatenate([rounded, moved], axis=-1)
    own = jnp.dot(inputs, stacked, preferred_element_type=jnp.float32) - reaction * field
    return own, rounded


def swapped(array, axis, partner):
    devices = lax.axis_size(axis)
    return lax.ppermute(array, axis, [(i, partner(i) % devices) for i in range(devices)])


def ring_order(devices):
    order = []
    for place in range(devices):
        chip = place // 2
        z = chip // 2
        x_hi = chip % 2 if z % 2 == 0 else 1 - chip % 2
        order.append((z * 2 + x_hi) * 2 + place % 2)
    return order


def exchange_faces(rounded):
    high = rounded[:, (NP - 1) * FACE :]
    low = rounded[:, :FACE]
    devices = lax.axis_size("gx")
    order = ring_order(devices)
    place = {device: index for index, device in enumerate(order)}
    far = lambda i: order[(place[i] + 1 if place[i] % 2 else place[i] - 1) % devices]
    odd = lax.axis_index("gx") % 2 == 1
    first = swapped(jnp.where(odd, low, high), "gx", lambda i: i ^ 1)
    second = swapped(jnp.where(odd, high, low), "gx", far)
    below = jnp.where(odd, first, second)
    above = jnp.where(odd, second, first)
    return jnp.concatenate([below, above], axis=-1)


def to_ring(array):
    order = ring_order(lax.axis_size("gx"))
    return lax.ppermute(array, "gx", [(slab, device) for slab, device in enumerate(order)])


def from_ring(array):
    order = ring_order(lax.axis_size("gx"))
    return lax.ppermute(array, "gx", [(device, slab) for slab, device in enumerate(order)])


def apply_operator(field, reaction, weights, x_lift, ny, nz):
    own, rounded = local_terms(field, reaction, weights, ny, nz)
    faces = exchange_faces(rounded)
    return own + jnp.dot(faces, x_lift, preferred_element_type=jnp.float32)


def gather_nodes(rows):
    nodes = lax.axis_size("node")
    me = lax.axis_index("node")
    swaps = [rows] + [swapped(rows, "node", lambda i, k=k: i ^ k) for k in range(1, nodes)]
    return swaps, me ^ jnp.arange(nodes)


def local(start_state, node_states, reaction_rates, volume, face_lift):
    node_times, weights_table = quadrature_table(M)
    shape = node_states.shape
    ny, nz, points = shape[-3], shape[-2], shape[-1]
    rows = ny * nz
    local_count = shape[0]
    first_node = lax.axis_index("node") * local_count
    all_weights = jnp.asarray(weights_table, jnp.float32)
    own_weights = lax.dynamic_slice_in_dim(all_weights, first_node, local_count, 0)
    all_scales = jnp.asarray(time_step * node_times, jnp.float32)
    own_scale = lax.dynamic_slice_in_dim(all_scales, first_node, local_count, 0)[0]

    weights = face_weights(volume, face_lift)
    x_lift = face_lift[: 2 * FACE]
    moved = to_ring(
        jnp.concatenate([node_states.reshape((rows, points)), reaction_rates.reshape((rows, points))], -1)
    )
    states = moved[:, :points]
    reaction = moved[:, points:]
    start = to_ring(start_state.reshape((rows, points)))
    for sweep_index in range(SWEEPS):
        slopes = apply_operator(states, reaction, weights, x_lift, ny, nz)
        slope_rows = slopes.astype(jnp.bfloat16)
        received, sources = gather_nodes(slope_rows)
        source_weights = jnp.take(own_weights[0], sources)
        stacked = jnp.stack(received).astype(jnp.float32)
        running_sum = jnp.sum(source_weights[:, None, None] * stacked, axis=0)
        fixed_part = start + time_step * running_sum - own_scale * slopes
        iterate = start + time_step * running_sum
        for inner_step in range(INNER - 1):
            iterate = fixed_part + own_scale * apply_operator(iterate, reaction, weights, x_lift, ny, nz)
        states = iterate
    return from_ring(states).reshape(shape)


def solution(mesh):
    in_specs = (
        P("gx", None, None, None),
        P("node", "gx", None, None, None),
        P("gx", None, None, None),
        P(),
        P(),
    )
    out_specs = P("node", "gx", None, None, None)
    return jax.shard_map(local, mesh=mesh, in_specs=in_specs, out_specs=out_specs, check_vma=False)
```

```python
import math

import jax
import jax.numpy as jnp
import numpy as np
from jax import lax
from jax.sharding import PartitionSpec as P

M = 8
NP = 8
SWEEPS = 2
INNER = 7
FACE = NP * NP


time_step = 0.45


def passed_along(array, axis, by):
    devices = lax.axis_size(axis)
    return lax.ppermute(array, axis, [(i, (i + by) % devices) for i in range(devices)])


def quadrature_table(node_count):
    roots_list = []
    for index in range(node_count):
        estimate = math.cos(math.pi * (index + 0.75) / (node_count + 0.5))
        for newton_step in range(60):
            previous, current = (1.0, estimate)
            for degree in range(2, node_count + 1):
                previous, current = (
                    current,
                    ((2 * degree - 1) * estimate * current - (degree - 1) * previous) / degree,
                )
            slope_value = node_count * (estimate * current - previous) / (estimate * estimate - 1.0)
            estimate = estimate - current / slope_value
        roots_list.append(0.5 * (estimate + 1.0))
    times_list = sorted(roots_list)
    weights_table = np.zeros((node_count, node_count))
    for column in range(node_count):
        coeffs = [1.0]
        scaling = 1.0
        for other in range(node_count):
            if other != column:
                point = times_list[other]
                widened = [0.0] * (len(coeffs) + 1)
                for power, entry in enumerate(coeffs):
                    widened[power + 1] += entry
                    widened[power] -= point * entry
                coeffs = widened
                scaling = scaling * (times_list[column] - point)
        for row in range(node_count):
            upper = times_list[row]
            total = 0.0
            for power, entry in enumerate(coeffs):
                total += entry / scaling * upper ** (power + 1) / (power + 1)
            weights_table[row, column] = total
    return (np.array(times_list), weights_table)


def face_selector(axis, value):
    a, b, c = np.meshgrid(np.arange(NP), np.arange(NP), np.arange(NP), indexing="ij")
    point = ((a * NP + b) * NP + c).reshape(-1)
    keep = [a, b, c][axis].reshape(-1) == value
    select = np.zeros((NP**3, FACE), np.float32)
    select[point[keep], np.arange(FACE)] = 1.0
    return select


def face_weights(volume, face_lift):
    picks = np.concatenate(
        [face_selector(axis, value) for axis, value in [(1, NP - 1), (1, 0), (2, NP - 1), (2, 0)]], axis=1
    ).argmax(axis=0)
    rows = lax.broadcasted_iota(jnp.int32, (NP**3, 4 * FACE), 0)
    select = (rows == jnp.asarray(picks, jnp.int32)[None, :]).astype(jnp.bfloat16)
    stacked = jnp.concatenate([volume, face_lift[2 * FACE :]], axis=0)
    return select, stacked


def local_terms(field, reaction, weights, ny, nz):
    select, stacked = weights
    rounded = field.astype(jnp.bfloat16)
    faces = jnp.dot(rounded, select, preferred_element_type=jnp.float32).astype(jnp.bfloat16)
    cube = faces.reshape((ny, nz, 4, FACE))
    moved = jnp.concatenate(
        [
            jnp.roll(cube[:, :, 0], 1, axis=0),
            jnp.roll(cube[:, :, 1], -1, axis=0),
            jnp.roll(cube[:, :, 2], 1, axis=1),
            jnp.roll(cube[:, :, 3], -1, axis=1),
        ],
        axis=-1,
    ).reshape((ny * nz, 4 * FACE))
    inputs = jnp.concatenate([rounded, moved], axis=-1)
    own = jnp.dot(inputs, stacked, preferred_element_type=jnp.float32) - reaction * field
    return own, rounded


def swapped(array, axis, partner):
    devices = lax.axis_size(axis)
    return lax.ppermute(array, axis, [(i, partner(i) % devices) for i in range(devices)])


def exchange_faces(rounded):
    both = jnp.concatenate([rounded[:, (NP - 1) * FACE :], rounded[:, :FACE]], axis=-1)
    first = swapped(both, "gx", lambda i: i ^ 1)
    second = swapped(both, "gx", lambda i: i + 1 if i % 2 else i - 1)
    return jnp.concatenate([first, second], axis=-1)


def parity_lift(face_lift):
    below = face_lift[:FACE]
    above = face_lift[FACE : 2 * FACE]
    zero = jnp.zeros_like(below)
    odd_rows = jnp.concatenate([below, zero, zero, above], axis=0)
    even_rows = jnp.concatenate([zero, above, below, zero], axis=0)
    return jnp.where(lax.axis_index("gx") % 2 == 1, odd_rows, even_rows)


def apply_operator(field, reaction, weights, x_lift, ny, nz):
    own, rounded = local_terms(field, reaction, weights, ny, nz)
    faces = exchange_faces(rounded)
    return own + jnp.dot(faces, x_lift, preferred_element_type=jnp.float32)


def gather_nodes(rows):
    nodes = lax.axis_size("node")
    me = lax.axis_index("node")
    swaps = [rows] + [swapped(rows, "node", lambda i, k=k: i ^ k) for k in range(1, nodes)]
    return swaps, me ^ jnp.arange(nodes)


def local(start_state, node_states, reaction_rates, volume, face_lift):
    node_times, weights_table = quadrature_table(M)
    shape = node_states.shape
    ny, nz, points = shape[-3], shape[-2], shape[-1]
    rows = ny * nz
    local_count = shape[0]
    first_node = lax.axis_index("node") * local_count
    all_weights = jnp.asarray(weights_table, jnp.float32)
    own_weights = lax.dynamic_slice_in_dim(all_weights, first_node, local_count, 0)
    all_scales = jnp.asarray(time_step * node_times, jnp.float32)
    own_scale = lax.dynamic_slice_in_dim(all_scales, first_node, local_count, 0)[0]

    weights = face_weights(volume, face_lift)
    x_lift = parity_lift(face_lift)
    start = start_state.reshape((rows, points))
    reaction = reaction_rates.reshape((rows, points))
    states = node_states.reshape((rows, points))
    for sweep_index in range(SWEEPS):
        slopes = apply_operator(states, reaction, weights, x_lift, ny, nz)
        slope_rows = slopes.astype(jnp.bfloat16)
        received, sources = gather_nodes(slope_rows)
        source_weights = jnp.take(own_weights[0], sources)
        stacked = jnp.stack(received).astype(jnp.float32)
        running_sum = jnp.sum(source_weights[:, None, None] * stacked, axis=0)
        fixed_part = start + time_step * running_sum - own_scale * slopes
        iterate = start + time_step * running_sum
        for inner_step in range(INNER - 1):
            iterate = fixed_part + own_scale * apply_operator(iterate, reaction, weights, x_lift, ny, nz)
        states = iterate
    return states.reshape(shape)


def solution(mesh):
    in_specs = (
        P("gx", None, None, None),
        P("node", "gx", None, None, None),
        P("gx", None, None, None),
        P(),
        P(),
    )
    out_specs = P("node", "gx", None, None, None)
    return jax.shard_map(local, mesh=mesh, in_specs=in_specs, out_specs=out_specs, check_vma=False)
```

```python
import math

import jax
import jax.numpy as jnp
import numpy as np
from jax import lax
from jax.sharding import PartitionSpec as P

M = 8
NP = 8
SWEEPS = 2
INNER = 7
FACE = NP * NP


time_step = 0.45


def passed_along(array, axis, by):
    devices = lax.axis_size(axis)
    return lax.ppermute(array, axis, [(i, (i + by) % devices) for i in range(devices)])


def quadrature_table(node_count):
    roots_list = []
    for index in range(node_count):
        estimate = math.cos(math.pi * (index + 0.75) / (node_count + 0.5))
        for newton_step in range(60):
            previous, current = (1.0, estimate)
            for degree in range(2, node_count + 1):
                previous, current = (
                    current,
                    ((2 * degree - 1) * estimate * current - (degree - 1) * previous) / degree,
                )
            slope_value = node_count * (estimate * current - previous) / (estimate * estimate - 1.0)
            estimate = estimate - current / slope_value
        roots_list.append(0.5 * (estimate + 1.0))
    times_list = sorted(roots_list)
    weights_table = np.zeros((node_count, node_count))
    for column in range(node_count):
        coeffs = [1.0]
        scaling = 1.0
        for other in range(node_count):
            if other != column:
                point = times_list[other]
                widened = [0.0] * (len(coeffs) + 1)
                for power, entry in enumerate(coeffs):
                    widened[power + 1] += entry
                    widened[power] -= point * entry
                coeffs = widened
                scaling = scaling * (times_list[column] - point)
        for row in range(node_count):
            upper = times_list[row]
            total = 0.0
            for power, entry in enumerate(coeffs):
                total += entry / scaling * upper ** (power + 1) / (power + 1)
            weights_table[row, column] = total
    return (np.array(times_list), weights_table)


def face_selector(axis, value):
    a, b, c = np.meshgrid(np.arange(NP), np.arange(NP), np.arange(NP), indexing="ij")
    point = ((a * NP + b) * NP + c).reshape(-1)
    keep = [a, b, c][axis].reshape(-1) == value
    select = np.zeros((NP**3, FACE), np.float32)
    select[point[keep], np.arange(FACE)] = 1.0
    return select


def face_weights(volume, face_lift):
    picks = np.concatenate(
        [face_selector(axis, value) for axis, value in [(1, NP - 1), (1, 0), (2, NP - 1), (2, 0)]], axis=1
    ).argmax(axis=0)
    rows = lax.broadcasted_iota(jnp.int32, (NP**3, 4 * FACE), 0)
    select = (rows == jnp.asarray(picks, jnp.int32)[None, :]).astype(jnp.bfloat16)
    stacked = jnp.concatenate([volume, face_lift[2 * FACE :]], axis=0)
    return select, stacked


def local_terms(field, reaction, weights, ny, nz):
    select, stacked = weights
    rounded = field.astype(jnp.bfloat16)
    faces = jnp.dot(rounded, select, preferred_element_type=jnp.float32).astype(jnp.bfloat16)
    z = lax.broadcasted_iota(jnp.int32, (ny * nz, FACE), 0) % nz
    z_low = faces[:, 2 * FACE : 3 * FACE]
    z_high = faces[:, 3 * FACE :]
    moved = jnp.concatenate(
        [
            jnp.roll(faces[:, :FACE], nz, axis=0),
            jnp.roll(faces[:, FACE : 2 * FACE], -nz, axis=0),
            jnp.where(z == 0, jnp.roll(z_low, 1 - nz, axis=0), jnp.roll(z_low, 1, axis=0)),
            jnp.where(z == nz - 1, jnp.roll(z_high, nz - 1, axis=0), jnp.roll(z_high, -1, axis=0)),
        ],
        axis=-1,
    )
    inputs = jnp.concatenate([rounded, moved], axis=-1)
    own = jnp.dot(inputs, stacked, preferred_element_type=jnp.float32) - reaction * field
    return own, rounded


def swapped(array, axis, partner):
    devices = lax.axis_size(axis)
    return lax.ppermute(array, axis, [(i, partner(i) % devices) for i in range(devices)])


def exchange_faces(rounded):
    high = rounded[:, (NP - 1) * FACE :]
    low = rounded[:, :FACE]
    odd = lax.axis_index("gx") % 2 == 1
    first = swapped(jnp.where(odd, low, high), "gx", lambda i: i ^ 1)
    second = swapped(jnp.where(odd, high, low), "gx", lambda i: i + 1 if i % 2 else i - 1)
    below = jnp.where(odd, first, second)
    above = jnp.where(odd, second, first)
    return jnp.concatenate([below, above], axis=-1)


def apply_operator(field, reaction, weights, x_lift, ny, nz):
    own, rounded = local_terms(field, reaction, weights, ny, nz)
    faces = exchange_faces(rounded)
    return own + jnp.dot(faces, x_lift, preferred_element_type=jnp.float32)


def gather_nodes(rows):
    nodes = lax.axis_size("node")
    me = lax.axis_index("node")
    swaps = [rows] + [swapped(rows, "node", lambda i, k=k: i ^ k) for k in range(1, nodes)]
    return swaps, me ^ jnp.arange(nodes)


def local(start_state, node_states, reaction_rates, volume, face_lift):
    node_times, weights_table = quadrature_table(M)
    shape = node_states.shape
    ny, nz, points = shape[-3], shape[-2], shape[-1]
    rows = ny * nz
    local_count = shape[0]
    first_node = lax.axis_index("node") * local_count
    all_weights = jnp.asarray(weights_table, jnp.float32)
    own_weights = lax.dynamic_slice_in_dim(all_weights, first_node, local_count, 0)
    all_scales = jnp.asarray(time_step * node_times, jnp.float32)
    own_scale = lax.dynamic_slice_in_dim(all_scales, first_node, local_count, 0)[0]

    weights = face_weights(volume, face_lift)
    x_lift = face_lift[: 2 * FACE]
    start = start_state.reshape((rows, points))
    reaction = reaction_rates.reshape((rows, points))
    states = node_states.reshape((rows, points))
    for sweep_index in range(SWEEPS):
        slopes = apply_operator(states, reaction, weights, x_lift, ny, nz)
        slope_rows = slopes.astype(jnp.bfloat16)
        received, sources = gather_nodes(slope_rows)
        source_weights = jnp.take(own_weights[0], sources)
        stacked = jnp.stack(received).astype(jnp.float32)
        running_sum = jnp.sum(source_weights[:, None, None] * stacked, axis=0)
        fixed_part = start + time_step * running_sum - own_scale * slopes
        iterate = start + time_step * running_sum
        for inner_step in range(INNER - 1):
            iterate = fixed_part + own_scale * apply_operator(iterate, reaction, weights, x_lift, ny, nz)
        states = iterate
    return states.reshape(shape)


def solution(mesh):
    in_specs = (
        P("gx", None, None, None),
        P("node", "gx", None, None, None),
        P("gx", None, None, None),
        P(),
        P(),
    )
    out_specs = P("node", "gx", None, None, None)
    return jax.shard_map(local, mesh=mesh, in_specs=in_specs, out_specs=out_specs, check_vma=False)
```

```python
import math

import jax
import jax.numpy as jnp
import numpy as np
from jax import lax
from jax.sharding import PartitionSpec as P

M = 8
NP = 8
SWEEPS = 2
INNER = 7
FACE = NP * NP


time_step = 0.45


def passed_along(array, axis, by):
    devices = lax.axis_size(axis)
    return lax.ppermute(array, axis, [(i, (i + by) % devices) for i in range(devices)])


def quadrature_table(node_count):
    roots_list = []
    for index in range(node_count):
        estimate = math.cos(math.pi * (index + 0.75) / (node_count + 0.5))
        for newton_step in range(60):
            previous, current = (1.0, estimate)
            for degree in range(2, node_count + 1):
                previous, current = (
                    current,
                    ((2 * degree - 1) * estimate * current - (degree - 1) * previous) / degree,
                )
            slope_value = node_count * (estimate * current - previous) / (estimate * estimate - 1.0)
            estimate = estimate - current / slope_value
        roots_list.append(0.5 * (estimate + 1.0))
    times_list = sorted(roots_list)
    weights_table = np.zeros((node_count, node_count))
    for column in range(node_count):
        coeffs = [1.0]
        scaling = 1.0
        for other in range(node_count):
            if other != column:
                point = times_list[other]
                widened = [0.0] * (len(coeffs) + 1)
                for power, entry in enumerate(coeffs):
                    widened[power + 1] += entry
                    widened[power] -= point * entry
                coeffs = widened
                scaling = scaling * (times_list[column] - point)
        for row in range(node_count):
            upper = times_list[row]
            total = 0.0
            for power, entry in enumerate(coeffs):
                total += entry / scaling * upper ** (power + 1) / (power + 1)
            weights_table[row, column] = total
    return (np.array(times_list), weights_table)


def face_selector(axis, value):
    a, b, c = np.meshgrid(np.arange(NP), np.arange(NP), np.arange(NP), indexing="ij")
    point = ((a * NP + b) * NP + c).reshape(-1)
    keep = [a, b, c][axis].reshape(-1) == value
    select = np.zeros((NP**3, FACE), np.float32)
    select[point[keep], np.arange(FACE)] = 1.0
    return select


def face_weights(volume, face_lift):
    select = np.concatenate(
        [face_selector(axis, value) for axis, value in [(1, NP - 1), (1, 0), (2, NP - 1), (2, 0)]], axis=1
    )
    stacked = jnp.concatenate([volume, face_lift[2 * FACE :]], axis=0)
    return jnp.asarray(select, jnp.bfloat16), stacked


def local_terms(field, reaction, weights, ny, nz):
    select, stacked = weights
    rounded = field.astype(jnp.bfloat16)
    faces = jnp.dot(rounded, select, preferred_element_type=jnp.float32).astype(jnp.bfloat16)
    cube = faces.reshape((ny, nz, 4, FACE))
    moved = jnp.concatenate(
        [
            jnp.roll(cube[:, :, 0], 1, axis=0),
            jnp.roll(cube[:, :, 1], -1, axis=0),
            jnp.roll(cube[:, :, 2], 1, axis=1),
            jnp.roll(cube[:, :, 3], -1, axis=1),
        ],
        axis=-1,
    ).reshape((ny * nz, 4 * FACE))
    inputs = jnp.concatenate([rounded, moved], axis=-1)
    own = jnp.dot(inputs, stacked, preferred_element_type=jnp.float32) - reaction * field
    return own, rounded


def swapped(array, axis, partner):
    devices = lax.axis_size(axis)
    return lax.ppermute(array, axis, [(i, partner(i) % devices) for i in range(devices)])


def exchange_faces(rounded):
    high = rounded[:, (NP - 1) * FACE :]
    low = rounded[:, :FACE]
    odd = lax.axis_index("gx") % 2 == 1
    first = swapped(jnp.where(odd, low, high), "gx", lambda i: i ^ 1)
    second = swapped(jnp.where(odd, high, low), "gx", lambda i: i + 1 if i % 2 else i - 1)
    below = jnp.where(odd, first, second)
    above = jnp.where(odd, second, first)
    return jnp.concatenate([below, above], axis=-1)


def apply_operator(field, reaction, weights, x_lift, ny, nz):
    own, rounded = local_terms(field, reaction, weights, ny, nz)
    faces = exchange_faces(rounded)
    return own + jnp.dot(faces, x_lift, preferred_element_type=jnp.float32)


def gather_nodes(rows):
    nodes = lax.axis_size("node")
    me = lax.axis_index("node")
    masks = [5, 4, 3, 7, 2, 6, 1] if nodes == 8 else list(range(1, nodes))
    swaps = [rows] + [swapped(rows, "node", lambda i, k=k: i ^ k) for k in masks]
    return swaps, me ^ jnp.asarray([0] + masks)


def local(start_state, node_states, reaction_rates, volume, face_lift):
    node_times, weights_table = quadrature_table(M)
    shape = node_states.shape
    ny, nz, points = shape[-3], shape[-2], shape[-1]
    rows = ny * nz
    local_count = shape[0]
    first_node = lax.axis_index("node") * local_count
    all_weights = jnp.asarray(weights_table, jnp.float32)
    own_weights = lax.dynamic_slice_in_dim(all_weights, first_node, local_count, 0)
    all_scales = jnp.asarray(time_step * node_times, jnp.float32)
    own_scale = lax.dynamic_slice_in_dim(all_scales, first_node, local_count, 0)[0]

    weights = face_weights(volume, face_lift)
    x_lift = face_lift[: 2 * FACE]
    start = start_state.reshape((rows, points))
    reaction = reaction_rates.reshape((rows, points))
    states = node_states.reshape((rows, points))
    for sweep_index in range(SWEEPS):
        slopes = apply_operator(states, reaction, weights, x_lift, ny, nz)
        slope_rows = slopes.astype(jnp.bfloat16)
        received, sources = gather_nodes(slope_rows)
        source_weights = jnp.take(own_weights[0], sources)
        stacked = jnp.stack(received).astype(jnp.float32)
        running_sum = jnp.sum(source_weights[:, None, None] * stacked, axis=0)
        fixed_part = start + time_step * running_sum - own_scale * slopes
        iterate = start + time_step * running_sum
        for inner_step in range(INNER - 1):
            iterate = fixed_part + own_scale * apply_operator(iterate, reaction, weights, x_lift, ny, nz)
        states = iterate
    return states.reshape(shape)


def solution(mesh):
    in_specs = (
        P("gx", None, None, None),
        P("node", "gx", None, None, None),
        P("gx", None, None, None),
        P(),
        P(),
    )
    out_specs = P("node", "gx", None, None, None)
    return jax.shard_map(local, mesh=mesh, in_specs=in_specs, out_specs=out_specs, check_vma=False)
```

```python
import math

import jax
import jax.numpy as jnp
import numpy as np
from jax import lax
from jax.sharding import PartitionSpec as P

M = 8
NP = 8
SWEEPS = 2
INNER = 7
FACE = NP * NP


time_step = 0.45


def passed_along(array, axis, by):
    devices = lax.axis_size(axis)
    return lax.ppermute(array, axis, [(i, (i + by) % devices) for i in range(devices)])


def quadrature_table(node_count):
    roots_list = []
    for index in range(node_count):
        estimate = math.cos(math.pi * (index + 0.75) / (node_count + 0.5))
        for newton_step in range(60):
            previous, current = (1.0, estimate)
            for degree in range(2, node_count + 1):
                previous, current = (
                    current,
                    ((2 * degree - 1) * estimate * current - (degree - 1) * previous) / degree,
                )
            slope_value = node_count * (estimate * current - previous) / (estimate * estimate - 1.0)
            estimate = estimate - current / slope_value
        roots_list.append(0.5 * (estimate + 1.0))
    times_list = sorted(roots_list)
    weights_table = np.zeros((node_count, node_count))
    for column in range(node_count):
        coeffs = [1.0]
        scaling = 1.0
        for other in range(node_count):
            if other != column:
                point = times_list[other]
                widened = [0.0] * (len(coeffs) + 1)
                for power, entry in enumerate(coeffs):
                    widened[power + 1] += entry
                    widened[power] -= point * entry
                coeffs = widened
                scaling = scaling * (times_list[column] - point)
        for row in range(node_count):
            upper = times_list[row]
            total = 0.0
            for power, entry in enumerate(coeffs):
                total += entry / scaling * upper ** (power + 1) / (power + 1)
            weights_table[row, column] = total
    return (np.array(times_list), weights_table)


def face_selector(axis, value):
    a, b, c = np.meshgrid(np.arange(NP), np.arange(NP), np.arange(NP), indexing="ij")
    point = ((a * NP + b) * NP + c).reshape(-1)
    keep = [a, b, c][axis].reshape(-1) == value
    select = np.zeros((NP**3, FACE), np.float32)
    select[point[keep], np.arange(FACE)] = 1.0
    return select


def face_weights(volume, face_lift):
    select = np.concatenate(
        [face_selector(axis, value) for axis, value in [(1, NP - 1), (1, 0), (2, NP - 1), (2, 0)]], axis=1
    )
    stacked = jnp.concatenate([volume, face_lift[2 * FACE :]], axis=0)
    return jnp.asarray(select, jnp.bfloat16), stacked


def local_terms(field, reaction, weights, ny, nz):
    select, stacked = weights
    rounded = field.astype(jnp.bfloat16)
    faces = jnp.dot(rounded, select, preferred_element_type=jnp.float32).astype(jnp.bfloat16)
    cube = faces.reshape((ny, nz, 4, FACE))
    moved = jnp.concatenate(
        [
            jnp.roll(cube[:, :, 0], 1, axis=0),
            jnp.roll(cube[:, :, 1], -1, axis=0),
            jnp.roll(cube[:, :, 2], 1, axis=1),
            jnp.roll(cube[:, :, 3], -1, axis=1),
        ],
        axis=-1,
    ).reshape((ny * nz, 4 * FACE))
    return jnp.concatenate([rounded, moved], axis=-1), rounded


def swapped(array, axis, partner):
    devices = lax.axis_size(axis)
    return lax.ppermute(array, axis, [(i, partner(i) % devices) for i in range(devices)])


def exchange_faces(rounded):
    high = rounded[:, (NP - 1) * FACE :]
    low = rounded[:, :FACE]
    odd = lax.axis_index("gx") % 2 == 1
    first = swapped(jnp.where(odd, low, high), "gx", lambda i: i ^ 1)
    second = swapped(jnp.where(odd, high, low), "gx", lambda i: i + 1 if i % 2 else i - 1)
    below = jnp.where(odd, first, second)
    above = jnp.where(odd, second, first)
    return jnp.concatenate([below, above], axis=-1)


def apply_operator(field, reaction, weights, x_lift, ny, nz):
    inputs, rounded = local_terms(field, reaction, weights, ny, nz)
    faces = exchange_faces(rounded)
    every = jnp.concatenate([inputs, faces], axis=-1)
    return jnp.dot(every, x_lift, preferred_element_type=jnp.float32) - reaction * field


def gather_nodes(rows):
    nodes = lax.axis_size("node")
    me = lax.axis_index("node")
    masks = [5, 4, 3, 7, 2, 6, 1] if nodes == 8 else list(range(1, nodes))
    swaps = [rows] + [swapped(rows, "node", lambda i, k=k: i ^ k) for k in masks]
    return swaps, me ^ jnp.asarray([0] + masks)


def local(start_state, node_states, reaction_rates, volume, face_lift):
    node_times, weights_table = quadrature_table(M)
    shape = node_states.shape
    ny, nz, points = shape[-3], shape[-2], shape[-1]
    rows = ny * nz
    local_count = shape[0]
    first_node = lax.axis_index("node") * local_count
    all_weights = jnp.asarray(weights_table, jnp.float32)
    own_weights = lax.dynamic_slice_in_dim(all_weights, first_node, local_count, 0)
    all_scales = jnp.asarray(time_step * node_times, jnp.float32)
    own_scale = lax.dynamic_slice_in_dim(all_scales, first_node, local_count, 0)[0]

    weights = face_weights(volume, face_lift)
    x_lift = jnp.concatenate([weights[1], face_lift[: 2 * FACE]], axis=0)
    start = start_state.reshape((rows, points))
    reaction = reaction_rates.reshape((rows, points))
    states = node_states.reshape((rows, points))
    for sweep_index in range(SWEEPS):
        slopes = apply_operator(states, reaction, weights, x_lift, ny, nz)
        slope_rows = slopes.astype(jnp.bfloat16)
        received, sources = gather_nodes(slope_rows)
        source_weights = jnp.take(own_weights[0], sources)
        stacked = jnp.stack(received).astype(jnp.float32)
        running_sum = jnp.sum(source_weights[:, None, None] * stacked, axis=0)
        fixed_part = start + time_step * running_sum - own_scale * slopes
        iterate = start + time_step * running_sum
        for inner_step in range(INNER - 1):
            iterate = fixed_part + own_scale * apply_operator(iterate, reaction, weights, x_lift, ny, nz)
        states = iterate
    return states.reshape(shape)


def solution(mesh):
    in_specs = (
        P("gx", None, None, None),
        P("node", "gx", None, None, None),
        P("gx", None, None, None),
        P(),
        P(),
    )
    out_specs = P("node", "gx", None, None, None)
    return jax.shard_map(local, mesh=mesh, in_specs=in_specs, out_specs=out_specs, check_vma=False)
```

```python
import math

import jax
import jax.numpy as jnp
import numpy as np
from jax import lax
from jax.sharding import PartitionSpec as P

M = 8
NP = 8
SWEEPS = 2
INNER = 7
FACE = NP * NP


time_step = 0.45


def passed_along(array, axis, by):
    devices = lax.axis_size(axis)
    return lax.ppermute(array, axis, [(i, (i + by) % devices) for i in range(devices)])


def quadrature_table(node_count):
    roots_list = []
    for index in range(node_count):
        estimate = math.cos(math.pi * (index + 0.75) / (node_count + 0.5))
        for newton_step in range(60):
            previous, current = (1.0, estimate)
            for degree in range(2, node_count + 1):
                previous, current = (
                    current,
                    ((2 * degree - 1) * estimate * current - (degree - 1) * previous) / degree,
                )
            slope_value = node_count * (estimate * current - previous) / (estimate * estimate - 1.0)
            estimate = estimate - current / slope_value
        roots_list.append(0.5 * (estimate + 1.0))
    times_list = sorted(roots_list)
    weights_table = np.zeros((node_count, node_count))
    for column in range(node_count):
        coeffs = [1.0]
        scaling = 1.0
        for other in range(node_count):
            if other != column:
                point = times_list[other]
                widened = [0.0] * (len(coeffs) + 1)
                for power, entry in enumerate(coeffs):
                    widened[power + 1] += entry
                    widened[power] -= point * entry
                coeffs = widened
                scaling = scaling * (times_list[column] - point)
        for row in range(node_count):
            upper = times_list[row]
            total = 0.0
            for power, entry in enumerate(coeffs):
                total += entry / scaling * upper ** (power + 1) / (power + 1)
            weights_table[row, column] = total
    return (np.array(times_list), weights_table)


def face_selector(axis, value):
    a, b, c = np.meshgrid(np.arange(NP), np.arange(NP), np.arange(NP), indexing="ij")
    point = ((a * NP + b) * NP + c).reshape(-1)
    keep = [a, b, c][axis].reshape(-1) == value
    select = np.zeros((NP**3, FACE), np.float32)
    select[point[keep], np.arange(FACE)] = 1.0
    return select


def face_weights(volume, face_lift):
    select = np.concatenate(
        [face_selector(axis, value) for axis, value in [(1, NP - 1), (1, 0), (2, NP - 1), (2, 0)]], axis=1
    )
    stacked = jnp.concatenate([volume, face_lift[2 * FACE :]], axis=0)
    return jnp.asarray(select, jnp.bfloat16), stacked


def local_terms(field, reaction, weights, ny, nz):
    select, stacked = weights
    rounded = field.astype(jnp.bfloat16)
    faces = jnp.dot(rounded, select, preferred_element_type=jnp.float32).astype(jnp.bfloat16)
    cube = faces.reshape((ny, nz, 4, FACE))
    moved = jnp.concatenate(
        [
            jnp.roll(cube[:, :, 0], 1, axis=0),
            jnp.roll(cube[:, :, 1], -1, axis=0),
            jnp.roll(cube[:, :, 2], 1, axis=1),
            jnp.roll(cube[:, :, 3], -1, axis=1),
        ],
        axis=-1,
    ).reshape((ny * nz, 4 * FACE))
    inputs = jnp.concatenate([rounded, moved], axis=-1)
    own = jnp.dot(inputs, stacked, preferred_element_type=jnp.float32) - reaction * field
    return own, rounded


def swapped(array, axis, partner):
    devices = lax.axis_size(axis)
    return lax.ppermute(array, axis, [(i, partner(i) % devices) for i in range(devices)])


def exchange_faces(rounded):
    high = rounded[:, (NP - 1) * FACE :]
    low = rounded[:, :FACE]
    odd = lax.axis_index("gx") % 2 == 1
    first = swapped(jnp.where(odd, low, high), "gx", lambda i: i ^ 1)
    second = swapped(jnp.where(odd, high, low), "gx", lambda i: i + 1 if i % 2 else i - 1)
    below = jnp.where(odd, first, second)
    above = jnp.where(odd, second, first)
    return jnp.concatenate([below, above], axis=-1)


def apply_operator(field, reaction, weights, x_lift, ny, nz):
    own, rounded = local_terms(field, reaction, weights, ny, nz)
    faces = exchange_faces(rounded)
    return own + jnp.dot(faces, x_lift, preferred_element_type=jnp.float32)


def gather_nodes(rows):
    nodes = lax.axis_size("node")
    me = lax.axis_index("node")
    pair = swapped(rows, "node", lambda i: i ^ 1)
    both = jnp.concatenate([rows, pair], axis=-1)
    width = rows.shape[-1]
    swaps, masks = [rows, pair], [0, 1]
    for k in [4, 6, 2] if nodes == 8 else range(2, nodes, 2):
        got = swapped(both, "node", lambda i, k=k: i ^ k)
        swaps += [got[:, :width], got[:, width:]]
        masks += [k, k ^ 1]
    return swaps, me ^ jnp.asarray(masks)


def local(start_state, node_states, reaction_rates, volume, face_lift):
    node_times, weights_table = quadrature_table(M)
    shape = node_states.shape
    ny, nz, points = shape[-3], shape[-2], shape[-1]
    rows = ny * nz
    local_count = shape[0]
    first_node = lax.axis_index("node") * local_count
    all_weights = jnp.asarray(weights_table, jnp.float32)
    own_weights = lax.dynamic_slice_in_dim(all_weights, first_node, local_count, 0)
    all_scales = jnp.asarray(time_step * node_times, jnp.float32)
    own_scale = lax.dynamic_slice_in_dim(all_scales, first_node, local_count, 0)[0]

    weights = face_weights(volume, face_lift)
    x_lift = face_lift[: 2 * FACE]
    start = start_state.reshape((rows, points))
    reaction = reaction_rates.reshape((rows, points))
    states = node_states.reshape((rows, points))
    for sweep_index in range(SWEEPS):
        slopes = apply_operator(states, reaction, weights, x_lift, ny, nz)
        slope_rows = slopes.astype(jnp.bfloat16)
        received, sources = gather_nodes(slope_rows)
        source_weights = jnp.take(own_weights[0], sources)
        stacked = jnp.stack(received).astype(jnp.float32)
        running_sum = jnp.sum(source_weights[:, None, None] * stacked, axis=0)
        fixed_part = start + time_step * running_sum - own_scale * slopes
        iterate = start + time_step * running_sum
        for inner_step in range(INNER - 1):
            iterate = fixed_part + own_scale * apply_operator(iterate, reaction, weights, x_lift, ny, nz)
        states = iterate
    return states.reshape(shape)


def solution(mesh):
    in_specs = (
        P("gx", None, None, None),
        P("node", "gx", None, None, None),
        P("gx", None, None, None),
        P(),
        P(),
    )
    out_specs = P("node", "gx", None, None, None)
    return jax.shard_map(local, mesh=mesh, in_specs=in_specs, out_specs=out_specs, check_vma=False)
```

```python
import math

import jax
import jax.numpy as jnp
import numpy as np
from jax import lax
from jax.sharding import PartitionSpec as P

M = 8
NP = 8
SWEEPS = 2
INNER = 7
FACE = NP * NP


time_step = 0.45


def passed_along(array, axis, by):
    devices = lax.axis_size(axis)
    return lax.ppermute(array, axis, [(i, (i + by) % devices) for i in range(devices)])


def quadrature_table(node_count):
    roots_list = []
    for index in range(node_count):
        estimate = math.cos(math.pi * (index + 0.75) / (node_count + 0.5))
        for newton_step in range(60):
            previous, current = (1.0, estimate)
            for degree in range(2, node_count + 1):
                previous, current = (
                    current,
                    ((2 * degree - 1) * estimate * current - (degree - 1) * previous) / degree,
                )
            slope_value = node_count * (estimate * current - previous) / (estimate * estimate - 1.0)
            estimate = estimate - current / slope_value
        roots_list.append(0.5 * (estimate + 1.0))
    times_list = sorted(roots_list)
    weights_table = np.zeros((node_count, node_count))
    for column in range(node_count):
        coeffs = [1.0]
        scaling = 1.0
        for other in range(node_count):
            if other != column:
                point = times_list[other]
                widened = [0.0] * (len(coeffs) + 1)
                for power, entry in enumerate(coeffs):
                    widened[power + 1] += entry
                    widened[power] -= point * entry
                coeffs = widened
                scaling = scaling * (times_list[column] - point)
        for row in range(node_count):
            upper = times_list[row]
            total = 0.0
            for power, entry in enumerate(coeffs):
                total += entry / scaling * upper ** (power + 1) / (power + 1)
            weights_table[row, column] = total
    return (np.array(times_list), weights_table)


def face_selector(axis, value):
    a, b, c = np.meshgrid(np.arange(NP), np.arange(NP), np.arange(NP), indexing="ij")
    point = ((a * NP + b) * NP + c).reshape(-1)
    keep = [a, b, c][axis].reshape(-1) == value
    select = np.zeros((NP**3, FACE), np.float32)
    select[point[keep], np.arange(FACE)] = 1.0
    return select


def face_weights(volume, face_lift):
    select = np.concatenate(
        [face_selector(axis, value) for axis, value in [(1, NP - 1), (1, 0), (2, NP - 1), (2, 0)]], axis=1
    )
    stacked = jnp.concatenate([volume, face_lift[2 * FACE :]], axis=0)
    return jnp.asarray(select, jnp.bfloat16), stacked


def local_terms(field, reaction, weights, ny, nz):
    select, stacked = weights
    rounded = field.astype(jnp.bfloat16)
    faces = jnp.dot(rounded, select, preferred_element_type=jnp.float32).astype(jnp.bfloat16)
    cube = faces.reshape((ny, nz, 4, FACE))
    moved = jnp.concatenate(
        [
            jnp.roll(cube[:, :, 0], 1, axis=0),
            jnp.roll(cube[:, :, 1], -1, axis=0),
            jnp.roll(cube[:, :, 2], 1, axis=1),
            jnp.roll(cube[:, :, 3], -1, axis=1),
        ],
        axis=-1,
    ).reshape((ny * nz, 4 * FACE))
    inputs = jnp.concatenate([rounded, moved], axis=-1)
    own = jnp.dot(inputs, stacked, preferred_element_type=jnp.float32) - reaction * field
    return own, rounded


def swapped(array, axis, partner):
    devices = lax.axis_size(axis)
    return lax.ppermute(array, axis, [(i, partner(i) % devices) for i in range(devices)])


def exchange_faces(rounded):
    high = rounded[:, (NP - 1) * FACE :]
    low = rounded[:, :FACE]
    odd = lax.axis_index("gx") % 2 == 1
    first = swapped(jnp.where(odd, low, high), "gx", lambda i: i ^ 1)
    second = swapped(jnp.where(odd, high, low), "gx", lambda i: i + 1 if i % 2 else i - 1)
    below = jnp.where(odd, first, second)
    above = jnp.where(odd, second, first)
    return jnp.concatenate([below, above], axis=-1)


def apply_operator(field, reaction, weights, x_lift, ny, nz):
    own, rounded = local_terms(field, reaction, weights, ny, nz)
    faces = exchange_faces(rounded)
    return own + jnp.dot(faces, x_lift, preferred_element_type=jnp.float32)


def gather_nodes(rows):
    nodes = lax.axis_size("node")
    me = lax.axis_index("node")
    masks = [5, 4, 3, 7, 2, 6, 1] if nodes == 8 else list(range(1, nodes))
    swaps = [rows] + [swapped(rows, "node", lambda i, k=k: i ^ k) for k in masks]
    return swaps, me ^ jnp.asarray([0] + masks)


def local(start_state, node_states, reaction_rates, volume, face_lift):
    node_times, weights_table = quadrature_table(M)
    shape = node_states.shape
    ny, nz, points = shape[-3], shape[-2], shape[-1]
    rows = ny * nz
    local_count = shape[0]
    first_node = lax.axis_index("node") * local_count
    all_weights = jnp.asarray(weights_table, jnp.float32)
    own_weights = lax.dynamic_slice_in_dim(all_weights, first_node, local_count, 0)
    all_scales = jnp.asarray(time_step * node_times, jnp.float32)
    own_scale = lax.dynamic_slice_in_dim(all_scales, first_node, local_count, 0)[0]

    weights = face_weights(volume, face_lift)
    x_lift = face_lift[: 2 * FACE]
    start = start_state.reshape((rows, points))
    reaction = reaction_rates.reshape((rows, points))
    states = node_states.reshape((rows, points))
    for sweep_index in range(SWEEPS):
        slopes = apply_operator(states, reaction, weights, x_lift, ny, nz)
        slope_rows = slopes.astype(jnp.bfloat16)
        received, sources = gather_nodes(slope_rows)
        source_weights = jnp.take(own_weights[0], sources)
        stacked = jnp.stack(received).astype(jnp.float32)
        running_sum = jnp.sum(source_weights[:, None, None] * stacked, axis=0)
        fixed_part = start + time_step * running_sum - own_scale * slopes
        iterate = start + time_step * running_sum
        for inner_step in range(INNER - 1):
            own, rounded = local_terms(iterate, reaction, weights, ny, nz)
            base = fixed_part + own_scale * own
            faces = exchange_faces(rounded)
            iterate = base + own_scale * jnp.dot(faces, x_lift, preferred_element_type=jnp.float32)
        states = iterate
    return states.reshape(shape)


def solution(mesh):
    in_specs = (
        P("gx", None, None, None),
        P("node", "gx", None, None, None),
        P("gx", None, None, None),
        P(),
        P(),
    )
    out_specs = P("node", "gx", None, None, None)
    return jax.shard_map(local, mesh=mesh, in_specs=in_specs, out_specs=out_specs, check_vma=False)
```

```python
import math

import jax
import jax.numpy as jnp
import numpy as np
from jax import lax
from jax.sharding import PartitionSpec as P

M = 8
NP = 8
SWEEPS = 2
INNER = 7
FACE = NP * NP


time_step = 0.45


def passed_along(array, axis, by):
    devices = lax.axis_size(axis)
    return lax.ppermute(array, axis, [(i, (i + by) % devices) for i in range(devices)])


def quadrature_table(node_count):
    roots_list = []
    for index in range(node_count):
        estimate = math.cos(math.pi * (index + 0.75) / (node_count + 0.5))
        for newton_step in range(60):
            previous, current = (1.0, estimate)
            for degree in range(2, node_count + 1):
                previous, current = (
                    current,
                    ((2 * degree - 1) * estimate * current - (degree - 1) * previous) / degree,
                )
            slope_value = node_count * (estimate * current - previous) / (estimate * estimate - 1.0)
            estimate = estimate - current / slope_value
        roots_list.append(0.5 * (estimate + 1.0))
    times_list = sorted(roots_list)
    weights_table = np.zeros((node_count, node_count))
    for column in range(node_count):
        coeffs = [1.0]
        scaling = 1.0
        for other in range(node_count):
            if other != column:
                point = times_list[other]
                widened = [0.0] * (len(coeffs) + 1)
                for power, entry in enumerate(coeffs):
                    widened[power + 1] += entry
                    widened[power] -= point * entry
                coeffs = widened
                scaling = scaling * (times_list[column] - point)
        for row in range(node_count):
            upper = times_list[row]
            total = 0.0
            for power, entry in enumerate(coeffs):
                total += entry / scaling * upper ** (power + 1) / (power + 1)
            weights_table[row, column] = total
    return (np.array(times_list), weights_table)


def face_selector(axis, value):
    a, b, c = np.meshgrid(np.arange(NP), np.arange(NP), np.arange(NP), indexing="ij")
    point = ((a * NP + b) * NP + c).reshape(-1)
    keep = [a, b, c][axis].reshape(-1) == value
    select = np.zeros((NP**3, FACE), np.float32)
    select[point[keep], np.arange(FACE)] = 1.0
    return select


def face_weights(volume, face_lift):
    select = np.concatenate(
        [face_selector(axis, value) for axis, value in [(1, NP - 1), (1, 0), (2, NP - 1), (2, 0)]], axis=1
    )
    stacked = jnp.concatenate([volume, face_lift[2 * FACE :]], axis=0)
    return jnp.asarray(select, jnp.bfloat16), stacked


def local_terms(field, reaction, weights, ny, nz):
    select, stacked = weights
    rounded = field.astype(jnp.bfloat16)
    faces = jnp.dot(rounded, select, preferred_element_type=jnp.float32).astype(jnp.bfloat16)
    cube = faces.reshape((ny, nz, 4, FACE))
    moved = jnp.concatenate(
        [
            jnp.roll(cube[:, :, 0], 1, axis=0),
            jnp.roll(cube[:, :, 1], -1, axis=0),
            jnp.roll(cube[:, :, 2], 1, axis=1),
            jnp.roll(cube[:, :, 3], -1, axis=1),
        ],
        axis=-1,
    ).reshape((ny * nz, 4 * FACE))
    inputs = jnp.concatenate([rounded, moved], axis=-1)
    own = jnp.dot(inputs, stacked, preferred_element_type=jnp.float32) - reaction * field
    return own, rounded


def swapped(array, axis, partner):
    devices = lax.axis_size(axis)
    return lax.ppermute(array, axis, [(i, partner(i) % devices) for i in range(devices)])


def exchange_faces(rounded):
    high = rounded[:, (NP - 1) * FACE :]
    low = rounded[:, :FACE]
    odd = lax.axis_index("gx") % 2 == 1
    first = swapped(jnp.where(odd, low, high), "gx", lambda i: i ^ 1)
    second = swapped(jnp.where(odd, high, low), "gx", lambda i: i + 1 if i % 2 else i - 1)
    below = jnp.where(odd, first, second)
    above = jnp.where(odd, second, first)
    return jnp.concatenate([below, above], axis=-1)


def apply_operator(field, reaction, weights, x_lift, ny, nz):
    own, rounded = local_terms(field, reaction, weights, ny, nz)
    faces = exchange_faces(rounded)
    return own + jnp.dot(faces, x_lift, preferred_element_type=jnp.float32)


def gather_nodes(rows):
    nodes = lax.axis_size("node")
    me = lax.axis_index("node")
    pair = swapped(rows, "node", lambda i: i ^ 1)
    both = jnp.concatenate([rows, pair], axis=-1)
    width = rows.shape[-1]
    swaps, masks = [rows, pair], [0, 1]
    for k in [4, 6, 2] if nodes == 8 else range(2, nodes, 2):
        got = swapped(both, "node", lambda i, k=k: i ^ k)
        swaps += [got[:, :width], got[:, width:]]
        masks += [k, k ^ 1]
    return swaps, me ^ jnp.asarray(masks)


def local(start_state, node_states, reaction_rates, volume, face_lift):
    node_times, weights_table = quadrature_table(M)
    shape = node_states.shape
    ny, nz, points = shape[-3], shape[-2], shape[-1]
    rows = ny * nz
    local_count = shape[0]
    first_node = lax.axis_index("node") * local_count
    all_weights = jnp.asarray(weights_table, jnp.float32)
    own_weights = lax.dynamic_slice_in_dim(all_weights, first_node, local_count, 0)
    all_scales = jnp.asarray(time_step * node_times, jnp.float32)
    own_scale = lax.dynamic_slice_in_dim(all_scales, first_node, local_count, 0)[0]

    weights = face_weights(volume, face_lift)
    x_lift = face_lift[: 2 * FACE]
    start = start_state.reshape((rows, points))
    reaction = reaction_rates.reshape((rows, points))
    states = node_states.reshape((rows, points))
    for sweep_index in range(SWEEPS):
        slopes = apply_operator(states, reaction, weights, x_lift, ny, nz)
        slope_rows = slopes.astype(jnp.bfloat16)
        received, sources = gather_nodes(slope_rows)
        source_weights = jnp.take(own_weights[0], sources)
        stacked = jnp.stack(received).astype(jnp.float32)
        running_sum = jnp.sum(source_weights[:, None, None] * stacked, axis=0)
        fixed_part = start + time_step * running_sum - own_scale * slopes
        iterate = start + time_step * running_sum
        for inner_step in range(INNER - 1):
            own, rounded = local_terms(iterate, reaction, weights, ny, nz)
            base = fixed_part + own_scale * own
            faces = exchange_faces(rounded)
            iterate = base + own_scale * jnp.dot(faces, x_lift, preferred_element_type=jnp.float32)
        states = iterate
    return states.reshape(shape)


def solution(mesh):
    in_specs = (
        P("gx", None, None, None),
        P("node", "gx", None, None, None),
        P("gx", None, None, None),
        P(),
        P(),
    )
    out_specs = P("node", "gx", None, None, None)
    return jax.shard_map(local, mesh=mesh, in_specs=in_specs, out_specs=out_specs, check_vma=False)
```
